256 devices in a mesh: win: 2 (over x_lo), seq: 128 (over x_hi, z, y, core).
Axes of the slice: x: 4 (x_hi: 2, x_lo: 2; x = x_hi * 2 + x_lo), y: 4, z: 8, core: 2. Of those that a mesh axis runs over, the one named last changes fastest.
Arguments:
- layer_input: bfloat16 [65536, 256], P(('win', 'seq')), parts along dimension 0, may hold values from -6 to 6
- w_in: bfloat16 [256, 768], replicated, may hold values from -0.375 to 0.375
- short_w: float32 [3, 768], replicated, may hold values from -3.5 to 3.5
- filters: float32 [2, 256, 32768], P(None, 'seq'), may hold values from -0.046875 to 0.046875
- filter_bias: float32 [2, 256], P(None, 'seq'), may hold values from -1 to 1
- w_out: bfloat16 [256, 256], replicated, may hold values from -0.375 to 0.375
Outputs:
- mixed: bfloat16 [65536, 256], P(('win', 'seq')), parts along dimension 0
The draws below stay inside these ranges and needn't reach their ends.
There are 2 independent parts, one for each index of `win`. The reference program is written for one: setup_inputs(seed, part) draws one part's arguments, and reference() takes and returns one part's arrays. A program takes and returns all parts, laid end to end along the dimension named above; an argument that names none is the same for every part. Nothing has to cross between parts.
All inputs are finite; a program needn't handle non-finite values.
Results may differ from the reference program's by a relative error of at most 0.018.
Values may be sent and summed in bfloat16 or wider, within the bound.
No kernel may reach another device: no remote copies, remote signals or barrier semaphores. Data moves between devices by JAX's collectives and lax.ppermute only.
A program may use at most 64 MiB of HBM per device.

```python
import jax
import jax.numpy as jnp

D = 256
ORDER = 2
SEQ = 32768


def steps_of(stream_key, extent, pieces, low, high):
    def one(position, parts):
        draws = jax.random.uniform(jax.random.fold_in(jax.random.fold_in(stream_key, 6), position), (parts,), jnp.float32, low / len(pieces), high / len(pieces))
        return jnp.repeat(jnp.exp(draws), extent[position] // parts).reshape((-1,) + (1,) * (len(extent) - position - 1))

    loudness = one(*pieces[0])
    for cut in pieces[1:]:
        loudness = loudness * one(*cut)
    return loudness


def noise(own_key, dims, width, most, shards=(), held_as=jnp.bfloat16):
    loudness = steps_of(own_key, dims, shards, -0.22, 0.18) if shards else 1.0
    values = jax.random.normal(own_key, dims, jnp.float32) * width * loudness
    return jnp.minimum(jnp.maximum(values, -most), most).astype(held_as)


def setup_inputs(seed: int = 0, part: int = 0) -> dict:
    arg_keys = jax.random.split(jax.random.key(seed), 7)
    own_keys = jax.random.split(jax.random.fold_in(arg_keys[6], part), 7)
    layer_input = noise(own_keys[0], (SEQ, D), 1.0, 6.0, ((0, 128),))
    w_in = noise(arg_keys[1], (D, 3 * D), D ** -0.5, 0.375)
    short_w = noise(arg_keys[2], (3, 3 * D), 3 ** -0.5, 3.5, (), jnp.float32)
    filters = noise(arg_keys[3], (ORDER, D, SEQ), (SEQ // 2) ** -0.5, 0.046875, ((1, 128),), jnp.float32)
    filter_bias = jnp.clip(jax.random.uniform(arg_keys[4], (ORDER, D), jnp.float32, -1.0, 1.0) * steps_of(arg_keys[4], (ORDER, D), ((1, 128),), -0.4, 0.0), -1.0, 1.0)
    w_out = noise(arg_keys[5], (D, D), D ** -0.5, 0.375)
    return {"layer_input": layer_input, "w_in": w_in, "short_w": short_w, "filters": filters, "filter_bias": filter_bias, "w_out": w_out}


def long_convolve(signal_in, filter_rows, bias_row):
    length = signal_in.shape[0]
    signal = signal_in.astype(jnp.float32)
    spectrum = jnp.fft.rfft(signal, n=2 * length, axis=0) * jnp.fft.rfft(filter_rows.T, n=2 * length, axis=0)
    convolved = jnp.fft.irfft(spectrum, n=2 * length, axis=0)[:length]
    return (convolved + bias_row[None, :] * signal).astype(jnp.bfloat16)


def reference(layer_input, w_in, short_w, filters, filter_bias, w_out):
    projected = jnp.dot(layer_input, w_in, preferred_element_type=jnp.float32).astype(jnp.bfloat16)
    padded = jnp.pad(projected.astype(jnp.float32), ((2, 0), (0, 0)))
    short = (short_w[0][None, :] * padded[2:] + short_w[1][None, :] * padded[1:-1] + short_w[2][None, :] * padded[:-2]).astype(jnp.bfloat16)
    gate_one = short[:, :D]
    gate_two = short[:, D:2 * D]
    value = short[:, 2 * D:]
    state_one = (gate_one.astype(jnp.float32) * long_convolve(value, filters[0], filter_bias[0]).astype(jnp.float32)).astype(jnp.bfloat16)
    state_two = (gate_two.astype(jnp.float32) * long_convolve(state_one, filters[1], filter_bias[1]).astype(jnp.float32)).astype(jnp.bfloat16)
    return jnp.dot(state_two, w_out, preferred_element_type=jnp.float32).astype(jnp.bfloat16)
```

```python
import math

import jax
import jax.numpy as jnp
from jax import lax
from jax.sharding import PartitionSpec as P

PRECISE = lax.Precision.HIGHEST


def shifted(block, axis, distance):
    devices = range(lax.axis_size(axis))
    route = [(i - distance, i) for i in devices if i - distance in devices]
    return lax.ppermute(block, axis, route)


def table_pair(table):
    upper = table.astype(jnp.bfloat16)
    lower = (table - upper.astype(jnp.float32)).astype(jnp.bfloat16)
    return (upper, lower)


def split_product(form, table, data):
    upper, lower = table_pair(table)
    return jnp.einsum(form, upper, data, preferred_element_type=jnp.float32) + jnp.einsum(
        form, lower, data, preferred_element_type=jnp.float32
    )


def dft_tables(length):
    places = jnp.arange(length, dtype=jnp.int32)
    angles = (
        -2.0 * math.pi / length * (places[:, None] * places[None, :] % length).astype(jnp.float32)
    )
    return (jnp.cos(angles), jnp.sin(angles))


def direct_dft(real_part, imag_part):
    length = real_part.shape[-1]
    cosine, sine_tab = dft_tables(length)
    out_real = jnp.einsum("...n,kn->...k", real_part, cosine, precision=PRECISE) - jnp.einsum(
        "...n,kn->...k", imag_part, sine_tab, precision=PRECISE
    )
    out_imag = jnp.einsum("...n,kn->...k", real_part, sine_tab, precision=PRECISE) + jnp.einsum(
        "...n,kn->...k", imag_part, cosine, precision=PRECISE
    )
    return (out_real, out_imag)


def transform(real_part, imag_part):
    length = real_part.shape[-1]
    if length <= 256:
        return direct_dft(real_part, imag_part)
    factor = math.gcd(length, min(128, length // 128))
    remain = length // factor
    leading = real_part.shape[:-1]
    real_grid = real_part.reshape(leading + (factor, remain))
    cosine, sine_tab = dft_tables(factor)
    if imag_part is None:
        section_real = split_product("kn,...ns->...ks", cosine, real_grid)
        section_imag = split_product("kn,...ns->...ks", sine_tab, real_grid)
    else:
        imag_grid = imag_part.reshape(leading + (factor, remain))
        section_real = jnp.einsum(
            "kn,...ns->...ks", cosine, real_grid, precision=PRECISE
        ) - jnp.einsum("kn,...ns->...ks", sine_tab, imag_grid, precision=PRECISE)
        section_imag = jnp.einsum(
            "kn,...ns->...ks", sine_tab, real_grid, precision=PRECISE
        ) + jnp.einsum("kn,...ns->...ks", cosine, imag_grid, precision=PRECISE)
    places = jnp.arange(factor, dtype=jnp.int32)
    columns = jnp.arange(remain, dtype=jnp.int32)
    twist_angle = (
        -2.0 * math.pi / length * (places[:, None] * columns[None, :] % length).astype(jnp.float32)
    )
    twist_cos = jnp.cos(twist_angle)
    twist_sin = jnp.sin(twist_angle)
    turned_real = section_real * twist_cos - section_imag * twist_sin
    turned_imag = section_real * twist_sin + section_imag * twist_cos
    inner_real, inner_imag = transform(turned_real, turned_imag)
    out_real = jnp.swapaxes(inner_real, -1, -2).reshape(leading + (length,))
    out_imag = jnp.swapaxes(inner_imag, -1, -2).reshape(leading + (length,))
    return (out_real, out_imag)


def long_convolve(signal_in, filter_rows, bias_row):
    channels, length = signal_in.shape
    signal_low = jnp.concatenate([signal_in, jnp.zeros((channels, length), jnp.bfloat16)], 1)
    padding = jnp.zeros((channels, length), jnp.float32)
    blank = jnp.zeros((channels, 2 * length), jnp.float32)
    signal_real, signal_imag = transform(signal_low, None)
    kernel_real, kernel_imag = transform(jnp.concatenate([filter_rows, padding], 1), blank)
    prod_real = signal_real * kernel_real - signal_imag * kernel_imag
    prod_imag = signal_real * kernel_imag + signal_imag * kernel_real
    back_real, back_imag = transform(prod_real, -prod_imag)
    convolved = back_real[:, :length] * (1.0 / (2 * length))
    return (convolved + bias_row[:, None] * signal_in.astype(jnp.float32)).astype(jnp.bfloat16)


def gated(gate_rows, conv_rows):
    return (gate_rows.astype(jnp.float32) * conv_rows.astype(jnp.float32)).astype(jnp.bfloat16)


def local(layer_input, w_in, short_w, filters, filter_bias, w_out):
    width = w_out.shape[0]
    groups = lax.axis_size("seq")
    per = width // groups
    projected = lax.dot_general(
        w_in, layer_input, (((0,), (1,)), ((), ())), preferred_element_type=jnp.float32
    ).astype(jnp.bfloat16)
    positions = projected.shape[1]
    grouped = jnp.swapaxes(projected.reshape(3, groups, per, positions), 0, 1)
    spread = lax.all_to_all(
        grouped.reshape(groups, 3 * per, positions), "seq", split_axis=0, concat_axis=2, tiled=True
    ).reshape(3 * per, groups * positions)
    me = lax.axis_index("seq")
    taps = lax.dynamic_slice_in_dim(short_w.reshape(3, 3, groups, per), me, 1, axis=2)
    taps = taps.reshape(3, 3 * per)
    extended = jnp.pad(spread.astype(jnp.float32), ((0, 0), (2, 0)))
    length = spread.shape[1]
    short = (
        taps[0][:, None] * extended[:, 2:]
        + taps[1][:, None] * extended[:, 1 : length + 1]
        + taps[2][:, None] * extended[:, :length]
    ).astype(jnp.bfloat16)
    gate_list = (short[:per], short[per : 2 * per])
    state = short[2 * per :]
    for order in range(2):
        convolved = long_convolve(state, filters[order], filter_bias[order])
        state = gated(gate_list[order], convolved)
    returned = lax.all_to_all(state, "seq", split_axis=1, concat_axis=0, tiled=True)
    output = lax.dot_general(
        returned, w_out, (((0,), (0,)), ((), ())), preferred_element_type=jnp.float32
    )
    return output.astype(jnp.bfloat16)


def solution(mesh):
    return jax.shard_map(
        local,
        mesh=mesh,
        in_specs=(P(("win", "seq"), None), P(), P(), P(None, "seq", None), P(None, "seq"), P()),
        out_specs=P(("win", "seq"), None),
        check_vma=False,
    )
```

```python
import math

import jax
import jax.numpy as jnp
from jax import lax
from jax.experimental import pallas as pl
from jax.experimental.pallas import tpu as pltpu
from jax.sharding import PartitionSpec as P

SIDE = 256


def halves(values):
    upper = values.astype(jnp.bfloat16)
    return upper, (values - upper.astype(jnp.float32)).astype(jnp.bfloat16)


def product(left, right):
    left_hi, left_lo = halves(left)
    right_hi, right_lo = halves(right)
    total = jnp.dot(left_hi, right_hi, preferred_element_type=jnp.float32)
    total = total + jnp.dot(left_lo, right_hi, preferred_element_type=jnp.float32)
    return total + jnp.dot(left_hi, right_lo, preferred_element_type=jnp.float32)


def make_tables():
    rows = lax.broadcasted_iota(jnp.int32, (SIDE, SIDE), 0)
    cols = lax.broadcasted_iota(jnp.int32, (SIDE, SIDE), 1)
    rows, cols = lax.optimization_barrier((rows, cols))
    step = -2.0 * math.pi / SIDE
    small = ((rows * cols) % SIDE).astype(jnp.float32) * step
    big = (rows * cols).astype(jnp.float32) * (step / SIDE)
    f_re, f_im = jnp.cos(small), jnp.sin(small)
    half = SIDE // 2
    left_fwd = jnp.concatenate([f_re[:, :half], f_im[:, :half]], 0)
    right_fwd = jnp.concatenate(
        [jnp.concatenate([f_re, f_im], 1), jnp.concatenate([-f_im, f_re], 1)], 0
    )
    right_inv = jnp.concatenate(
        [jnp.concatenate([f_re, -f_im], 1), jnp.concatenate([f_im, f_re], 1)], 0
    )
    left_inv = jnp.concatenate([f_re[:half], f_im[:half]], 1)
    return left_fwd, right_fwd, right_inv, left_inv, jnp.cos(big), jnp.sin(big)


def spectrum(rows_in, left_fwd, right_fwd, tw_re, tw_im):
    stacked = product(left_fwd, rows_in)
    b_re, b_im = stacked[:SIDE], stacked[SIDE:]
    t_re = b_re * tw_re - b_im * tw_im
    t_im = b_re * tw_im + b_im * tw_re
    return product(jnp.concatenate([t_re, t_im], 1), right_fwd)


def convolve(sig, filt, bias, tabs):
    left_fwd, right_fwd, right_inv, left_inv, tw_re, tw_im = tabs
    signal = sig.astype(jnp.float32)
    s_spec = spectrum(signal, left_fwd, right_fwd, tw_re, tw_im)
    f_spec = spectrum(filt, left_fwd, right_fwd, tw_re, tw_im)
    s_re, s_im = s_spec[:, :SIDE], s_spec[:, SIDE:]
    f_re, f_im = f_spec[:, :SIDE], f_spec[:, SIDE:]
    p_re = s_re * f_re - s_im * f_im
    p_im = s_re * f_im + s_im * f_re
    d = product(jnp.concatenate([p_re, p_im], 1), right_inv)
    d_re, d_im = d[:, :SIDE], d[:, SIDE:]
    e_re = d_re * tw_re + d_im * tw_im
    e_im = d_im * tw_re - d_re * tw_im
    back = product(left_inv, jnp.concatenate([e_re, e_im], 0))
    scale = 1.0 / (SIDE * SIDE)
    return (back * scale + bias * signal).astype(jnp.bfloat16)


def chain_kernel(short_ref, filt_ref, bias_ref, lf_ref, rf_ref, ri_ref, li_ref, twr_ref, twi_ref, out_ref):
    channel = pl.program_id(0)
    tabs = (lf_ref[...], rf_ref[...], ri_ref[...], li_ref[...], twr_ref[...], twi_ref[...])
    state = short_ref[2, 0]
    for order in range(2):
        conv = convolve(state, filt_ref[order, 0], bias_ref[order, channel], tabs)
        state = (short_ref[order, 0].astype(jnp.float32) * conv.astype(jnp.float32)).astype(jnp.bfloat16)
    out_ref[0] = state


def chain(short, filters, bias):
    per = short.shape[1]
    half = SIDE // 2
    tabs = make_tables()
    full = lambda shape: pl.BlockSpec(shape, lambda c: (0,) * len(shape))
    return pl.pallas_call(
        chain_kernel,
        grid=(per,),
        in_specs=[
            pl.BlockSpec((3, 1, half, SIDE), lambda c: (0, c, 0, 0)),
            pl.BlockSpec((2, 1, half, SIDE), lambda c: (0, c, 0, 0)),
            pl.BlockSpec(memory_space=pltpu.SMEM),
            full((2 * SIDE, half)),
            full((2 * SIDE, 2 * SIDE)),
            full((2 * SIDE, 2 * SIDE)),
            full((half, 2 * SIDE)),
            full((SIDE, SIDE)),
            full((SIDE, SIDE)),
        ],
        out_specs=pl.BlockSpec((1, half, SIDE), lambda c: (c, 0, 0)),
        out_shape=jax.ShapeDtypeStruct((per, half, SIDE), jnp.bfloat16),
        compiler_params=pltpu.CompilerParams(vmem_limit_bytes=48 * 1024 * 1024),
    )(short, filters, bias, *tabs)


def local(layer_input, w_in, short_w, filters, filter_bias, w_out):
    width = w_out.shape[0]
    groups = lax.axis_size("seq")
    per = width // groups
    projected = lax.dot_general(
        w_in, layer_input, (((0,), (1,)), ((), ())), preferred_element_type=jnp.float32
    ).astype(jnp.bfloat16)
    positions = projected.shape[1]
    grouped = jnp.swapaxes(projected.reshape(3, groups, per, positions), 0, 1)
    spread = lax.all_to_all(
        grouped.reshape(groups, 3 * per, positions), "seq", split_axis=0, concat_axis=2, tiled=True
    ).reshape(3 * per, groups * positions)
    me = lax.axis_index("seq")
    taps = lax.dynamic_slice_in_dim(short_w.reshape(3, 3, groups, per), me, 1, axis=2)
    taps = taps.reshape(3, 3 * per)
    extended = jnp.pad(spread.astype(jnp.float32), ((0, 0), (2, 0)))
    length = spread.shape[1]
    short = (
        taps[0][:, None] * extended[:, 2:]
        + taps[1][:, None] * extended[:, 1 : length + 1]
        + taps[2][:, None] * extended[:, :length]
    ).astype(jnp.bfloat16)
    half = SIDE // 2
    state = chain(
        short.reshape(3, per, half, SIDE),
        filters.reshape(2, per, half, SIDE),
        filter_bias,
    ).reshape(per, length)
    returned = lax.all_to_all(state, "seq", split_axis=1, concat_axis=0, tiled=True)
    output = lax.dot_general(
        returned, w_out, (((0,), (0,)), ((), ())), preferred_element_type=jnp.float32
    )
    return output.astype(jnp.bfloat16)


def solution(mesh):
    return jax.shard_map(
        local,
        mesh=mesh,
        in_specs=(P(("win", "seq"), None), P(), P(), P(None, "seq", None), P(None, "seq"), P()),
        out_specs=P(("win", "seq"), None),
        check_vma=False,
    )
```

```python
import math

import jax
import jax.numpy as jnp
from jax import lax
from jax.experimental import pallas as pl
from jax.experimental.pallas import tpu as pltpu
from jax.sharding import PartitionSpec as P

SIDE = 256


def halves(values):
    upper = values.astype(jnp.bfloat16)
    return upper, (values - upper.astype(jnp.float32)).astype(jnp.bfloat16)


def product(left, right):
    left_hi, left_lo = halves(left)
    right_hi, right_lo = halves(right)
    total = jnp.dot(left_hi, right_hi, preferred_element_type=jnp.float32)
    total = total + jnp.dot(left_lo, right_hi, preferred_element_type=jnp.float32)
    return total + jnp.dot(left_hi, right_lo, preferred_element_type=jnp.float32)


def single(left, right):
    return jnp.dot(
        left.astype(jnp.bfloat16), right.astype(jnp.bfloat16), preferred_element_type=jnp.float32
    )


def make_tables():
    rows = lax.broadcasted_iota(jnp.int32, (SIDE, SIDE), 0)
    cols = lax.broadcasted_iota(jnp.int32, (SIDE, SIDE), 1)
    rows, cols = lax.optimization_barrier((rows, cols))
    step = -2.0 * math.pi / SIDE
    small = ((rows * cols) % SIDE).astype(jnp.float32) * step
    big = (rows * cols).astype(jnp.float32) * (step / SIDE)
    f_re, f_im = jnp.cos(small), jnp.sin(small)
    half = SIDE // 2
    left_fwd = jnp.concatenate([f_re[:, :half], f_im[:, :half]], 0)
    right_fwd = jnp.concatenate(
        [jnp.concatenate([f_re, f_im], 1), jnp.concatenate([-f_im, f_re], 1)], 0
    )
    right_inv = jnp.concatenate(
        [jnp.concatenate([f_re, -f_im], 1), jnp.concatenate([f_im, f_re], 1)], 0
    )
    left_inv = jnp.concatenate([f_re[:half], f_im[:half]], 1)
    return left_fwd, right_fwd, right_inv, left_inv, jnp.cos(big), jnp.sin(big)


def spectrum(rows_in, left_fwd, right_fwd, tw_re, tw_im, mul):
    stacked = mul(left_fwd, rows_in)
    b_re, b_im = stacked[:SIDE], stacked[SIDE:]
    t_re = b_re * tw_re - b_im * tw_im
    t_im = b_re * tw_im + b_im * tw_re
    return mul(jnp.concatenate([t_re, t_im], 1), right_fwd)


def filter_kernel(filt_ref, lf_ref, rf_ref, twr_ref, twi_ref, out_ref):
    out_ref[0, 0] = spectrum(
        filt_ref[0, 0], lf_ref[...], rf_ref[...], twr_ref[...], twi_ref[...], product
    )


def filter_spectra(filters, tabs):
    left_fwd, right_fwd, _, _, tw_re, tw_im = tabs
    orders, per = filters.shape[:2]
    half = SIDE // 2
    full = lambda shape: pl.BlockSpec(shape, lambda o, c: (0,) * len(shape))
    return pl.pallas_call(
        filter_kernel,
        grid=(orders, per),
        in_specs=[
            pl.BlockSpec((1, 1, half, SIDE), lambda o, c: (o, c, 0, 0)),
            full((2 * SIDE, half)),
            full((2 * SIDE, 2 * SIDE)),
            full((SIDE, SIDE)),
            full((SIDE, SIDE)),
        ],
        out_specs=pl.BlockSpec((1, 1, SIDE, 2 * SIDE), lambda o, c: (o, c, 0, 0)),
        out_shape=jax.ShapeDtypeStruct((orders, per, SIDE, 2 * SIDE), jnp.float32),
        compiler_params=pltpu.CompilerParams(vmem_limit_bytes=48 * 1024 * 1024),
    )(filters, left_fwd, right_fwd, tw_re, tw_im)


def convolve(sig, f_spec, bias, tabs):
    left_fwd, right_fwd, right_inv, left_inv, tw_re, tw_im = tabs
    signal = sig.astype(jnp.float32)
    s_spec = spectrum(sig, left_fwd, right_fwd, tw_re, tw_im, single)
    s_re, s_im = s_spec[:, :SIDE], s_spec[:, SIDE:]
    f_re, f_im = f_spec[:, :SIDE], f_spec[:, SIDE:]
    p_re = s_re * f_re - s_im * f_im
    p_im = s_re * f_im + s_im * f_re
    d = single(jnp.concatenate([p_re, p_im], 1), right_inv)
    d_re, d_im = d[:, :SIDE], d[:, SIDE:]
    e_re = d_re * tw_re + d_im * tw_im
    e_im = d_im * tw_re - d_re * tw_im
    back = single(left_inv, jnp.concatenate([e_re, e_im], 0))
    scale = 1.0 / (SIDE * SIDE)
    return (back * scale + bias * signal).astype(jnp.bfloat16)


def chain_kernel(short_ref, spec_ref, bias_ref, lf_ref, rf_ref, ri_ref, li_ref, twr_ref, twi_ref, out_ref):
    channel = pl.program_id(0)
    tabs = (lf_ref[...], rf_ref[...], ri_ref[...], li_ref[...], twr_ref[...], twi_ref[...])
    state = short_ref[2, 0]
    for order in range(2):
        conv = convolve(state, spec_ref[order, 0], bias_ref[order, channel], tabs)
        state = (short_ref[order, 0].astype(jnp.float32) * conv.astype(jnp.float32)).astype(jnp.bfloat16)
    out_ref[0] = state


def chain(short, spectra, bias, tabs):
    per = short.shape[1]
    half = SIDE // 2
    left_fwd, right_fwd, right_inv, left_inv, tw_re, tw_im = tabs
    low = lambda t: t.astype(jnp.bfloat16)
    full = lambda shape: pl.BlockSpec(shape, lambda c: (0,) * len(shape))
    return pl.pallas_call(
        chain_kernel,
        grid=(per,),
        in_specs=[
            pl.BlockSpec((3, 1, half, SIDE), lambda c: (0, c, 0, 0)),
            pl.BlockSpec((2, 1, SIDE, 2 * SIDE), lambda c: (0, c, 0, 0)),
            pl.BlockSpec(memory_space=pltpu.SMEM),
            full((2 * SIDE, half)),
            full((2 * SIDE, 2 * SIDE)),
            full((2 * SIDE, 2 * SIDE)),
            full((half, 2 * SIDE)),
            full((SIDE, SIDE)),
            full((SIDE, SIDE)),
        ],
        out_specs=pl.BlockSpec((1, half, SIDE), lambda c: (c, 0, 0)),
        out_shape=jax.ShapeDtypeStruct((per, half, SIDE), jnp.bfloat16),
        compiler_params=pltpu.CompilerParams(vmem_limit_bytes=48 * 1024 * 1024),
    )(short, spectra, bias, low(left_fwd), low(right_fwd), low(right_inv), low(left_inv), tw_re, tw_im)


def local(layer_input, w_in, short_w, filters, filter_bias, w_out):
    width = w_out.shape[0]
    groups = lax.axis_size("seq")
    per = width // groups
    projected = lax.dot_general(
        w_in, layer_input, (((0,), (1,)), ((), ())), preferred_element_type=jnp.float32
    ).astype(jnp.bfloat16)
    positions = projected.shape[1]
    grouped = jnp.swapaxes(projected.reshape(3, groups, per, positions), 0, 1)
    tabs = make_tables()
    spectra = filter_spectra(filters.reshape(2, per, SIDE // 2, SIDE), tabs)
    spread = lax.all_to_all(
        grouped.reshape(groups, 3 * per, positions), "seq", split_axis=0, concat_axis=2, tiled=True
    ).reshape(3 * per, groups * positions)
    me = lax.axis_index("seq")
    taps = lax.dynamic_slice_in_dim(short_w.reshape(3, 3, groups, per), me, 1, axis=2)
    taps = taps.reshape(3, 3 * per)
    extended = jnp.pad(spread.astype(jnp.float32), ((0, 0), (2, 0)))
    length = spread.shape[1]
    short = (
        taps[0][:, None] * extended[:, 2:]
        + taps[1][:, None] * extended[:, 1 : length + 1]
        + taps[2][:, None] * extended[:, :length]
    ).astype(jnp.bfloat16)
    half = SIDE // 2
    state = chain(
        short.reshape(3, per, half, SIDE),
        spectra,
        filter_bias,
        tabs,
    ).reshape(per, length)
    returned = lax.all_to_all(state, "seq", split_axis=1, concat_axis=0, tiled=True)
    output = lax.dot_general(
        returned, w_out, (((0,), (0,)), ((), ())), preferred_element_type=jnp.float32
    )
    return output.astype(jnp.bfloat16)


def solution(mesh):
    return jax.shard_map(
        local,
        mesh=mesh,
        in_specs=(P(("win", "seq"), None), P(), P(), P(None, "seq", None), P(None, "seq"), P()),
        out_specs=P(("win", "seq"), None),
        check_vma=False,
    )
```

```python
import math

import jax
import jax.numpy as jnp
from jax import lax
from jax.experimental import pallas as pl
from jax.experimental.pallas import tpu as pltpu
from jax.sharding import PartitionSpec as P

SIDE = 256


def halves(values):
    upper = values.astype(jnp.bfloat16)
    return upper, (values - upper.astype(jnp.float32)).astype(jnp.bfloat16)


def product(left, right):
    left_hi, left_lo = halves(left)
    right_hi, right_lo = halves(right)
    total = jnp.dot(left_hi, right_hi, preferred_element_type=jnp.float32)
    total = total + jnp.dot(left_lo, right_hi, preferred_element_type=jnp.float32)
    return total + jnp.dot(left_hi, right_lo, preferred_element_type=jnp.float32)


def single(left, right):
    return jnp.dot(
        left.astype(jnp.bfloat16), right.astype(jnp.bfloat16), preferred_element_type=jnp.float32
    )


def make_tables():
    rows = lax.broadcasted_iota(jnp.int32, (SIDE, SIDE), 0)
    cols = lax.broadcasted_iota(jnp.int32, (SIDE, SIDE), 1)
    rows, cols = lax.optimization_barrier((rows, cols))
    step = -2.0 * math.pi / SIDE
    small = ((rows * cols) % SIDE).astype(jnp.float32) * step
    big = (rows * cols).astype(jnp.float32) * (step / SIDE)
    f_re, f_im = jnp.cos(small), jnp.sin(small)
    half = SIDE // 2
    left_fwd = jnp.concatenate([f_re[:, :half], f_im[:, :half]], 0)
    right_fwd = jnp.concatenate(
        [jnp.concatenate([f_re, f_im], 1), jnp.concatenate([-f_im, f_re], 1)], 0
    )
    right_inv = jnp.concatenate(
        [jnp.concatenate([f_re, -f_im], 1), jnp.concatenate([f_im, f_re], 1)], 0
    )
    left_inv = jnp.concatenate([f_re[:half], f_im[:half]], 1)
    return left_fwd, right_fwd, right_inv, left_inv, jnp.cos(big), jnp.sin(big)


def spectrum(rows_in, left_fwd, right_fwd, tw_re, tw_im, mul):
    stacked = mul(left_fwd, rows_in)
    b_re, b_im = stacked[:SIDE], stacked[SIDE:]
    t_re = b_re * tw_re - b_im * tw_im
    t_im = b_re * tw_im + b_im * tw_re
    return mul(jnp.concatenate([t_re, t_im], 1), right_fwd)


def filter_kernel(filt_ref, lf_ref, rf_ref, twr_ref, twi_ref, out_ref):
    out_ref[0, 0] = spectrum(
        filt_ref[0, 0], lf_ref[...], rf_ref[...], twr_ref[...], twi_ref[...], product
    )


def filter_spectra(filters, tabs):
    left_fwd, right_fwd, _, _, tw_re, tw_im = tabs
    orders, per = filters.shape[:2]
    half = SIDE // 2
    full = lambda shape: pl.BlockSpec(shape, lambda o, c: (0,) * len(shape))
    return pl.pallas_call(
        filter_kernel,
        grid=(orders, per),
        in_specs=[
            pl.BlockSpec((1, 1, half, SIDE), lambda o, c: (o, c, 0, 0)),
            full((2 * SIDE, half)),
            full((2 * SIDE, 2 * SIDE)),
            full((SIDE, SIDE)),
            full((SIDE, SIDE)),
        ],
        out_specs=pl.BlockSpec((1, 1, SIDE, 2 * SIDE), lambda o, c: (o, c, 0, 0)),
        out_shape=jax.ShapeDtypeStruct((orders, per, SIDE, 2 * SIDE), jnp.float32),
        compiler_params=pltpu.CompilerParams(vmem_limit_bytes=48 * 1024 * 1024),
    )(filters, left_fwd, right_fwd, tw_re, tw_im)


def convolve(sig, f_spec, bias, tabs):
    left_fwd, right_fwd, right_inv, left_inv, tw_re, tw_im = tabs
    signal = sig.astype(jnp.float32)
    s_spec = spectrum(sig, left_fwd, right_fwd, tw_re, tw_im, single)
    s_re, s_im = s_spec[:, :SIDE], s_spec[:, SIDE:]
    f_re, f_im = f_spec[:, :SIDE], f_spec[:, SIDE:]
    p_re = s_re * f_re - s_im * f_im
    p_im = s_re * f_im + s_im * f_re
    d = single(jnp.concatenate([p_re, p_im], 1), right_inv)
    d_re, d_im = d[:, :SIDE], d[:, SIDE:]
    e_re = d_re * tw_re + d_im * tw_im
    e_im = d_im * tw_re - d_re * tw_im
    back = single(left_inv, jnp.concatenate([e_re, e_im], 0))
    scale = 1.0 / (SIDE * SIDE)
    return (back * scale + bias * signal).astype(jnp.bfloat16)


def shift_tables():
    big_r = lax.broadcasted_iota(jnp.int32, (2 * SIDE, 2 * SIDE), 0)
    big_c = lax.broadcasted_iota(jnp.int32, (2 * SIDE, 2 * SIDE), 1)
    small_r = lax.broadcasted_iota(jnp.int32, (SIDE // 2, SIDE // 2), 0)
    small_c = lax.broadcasted_iota(jnp.int32, (SIDE // 2, SIDE // 2), 1)
    big_r, big_c, small_r, small_c = lax.optimization_barrier((big_r, big_c, small_r, small_c))
    upper = big_r < SIDE
    source = jnp.where(upper, big_r, big_r - 2 * SIDE)
    lag = jnp.where(big_c < SIDE, 1, 2)
    target = jnp.where(big_c < SIDE, big_c, big_c - SIDE)
    shifts = (source + lag == target).astype(jnp.bfloat16)
    rows = (small_c + 1 == small_r).astype(jnp.bfloat16)
    return shifts, rows


def chain_kernel(
    proj_ref, spec_ref, bias_ref, taps_ref, sh_ref, rw_ref,
    lf_ref, rf_ref, ri_ref, li_ref, twr_ref, twi_ref, out_ref,
):
    channel = pl.program_id(0)
    tabs = (lf_ref[...], rf_ref[...], ri_ref[...], li_ref[...], twr_ref[...], twi_ref[...])
    streams = []
    for stream in range(3):
        p = proj_ref[stream, 0]
        q = jnp.dot(rw_ref[...], p, preferred_element_type=jnp.float32).astype(jnp.bfloat16)
        moved = jnp.dot(
            jnp.concatenate([p, q], 1), sh_ref[...], preferred_element_type=jnp.float32
        )
        short = (
            taps_ref[stream, channel] * p.astype(jnp.float32)
            + taps_ref[3 + stream, channel] * moved[:, :SIDE]
            + taps_ref[6 + stream, channel] * moved[:, SIDE:]
        )
        streams.append(short.astype(jnp.bfloat16))
    state = streams[2]
    for order in range(2):
        conv = convolve(state, spec_ref[order, 0], bias_ref[order, channel], tabs)
        state = (streams[order].astype(jnp.float32) * conv.astype(jnp.float32)).astype(jnp.bfloat16)
    out_ref[0] = state


def chain(proj, spectra, bias, taps, tabs):
    per = proj.shape[1]
    half = SIDE // 2
    left_fwd, right_fwd, right_inv, left_inv, tw_re, tw_im = tabs
    shifts, rows = shift_tables()
    low = lambda t: t.astype(jnp.bfloat16)
    full = lambda shape: pl.BlockSpec(shape, lambda c: (0,) * len(shape))
    return pl.pallas_call(
        chain_kernel,
        grid=(per,),
        in_specs=[
            pl.BlockSpec((3, 1, half, SIDE), lambda c: (0, c, 0, 0)),
            pl.BlockSpec((2, 1, SIDE, 2 * SIDE), lambda c: (0, c, 0, 0)),
            pl.BlockSpec(memory_space=pltpu.SMEM),
            pl.BlockSpec(memory_space=pltpu.SMEM),
            full((2 * SIDE, 2 * SIDE)),
            full((half, half)),
            full((2 * SIDE, half)),
            full((2 * SIDE, 2 * SIDE)),
            full((2 * SIDE, 2 * SIDE)),
            full((half, 2 * SIDE)),
            full((SIDE, SIDE)),
            full((SIDE, SIDE)),
        ],
        out_specs=pl.BlockSpec((1, half, SIDE), lambda c: (c, 0, 0)),
        out_shape=jax.ShapeDtypeStruct((per, half, SIDE), jnp.bfloat16),
        compiler_params=pltpu.CompilerParams(vmem_limit_bytes=48 * 1024 * 1024),
    )(
        proj, spectra, bias, taps, shifts, rows,
        low(left_fwd), low(right_fwd), low(right_inv), low(left_inv), tw_re, tw_im,
    )


def local(layer_input, w_in, short_w, filters, filter_bias, w_out):
    width = w_out.shape[0]
    groups = lax.axis_size("seq")
    per = width // groups
    projected = lax.dot_general(
        w_in, layer_input, (((0,), (1,)), ((), ())), preferred_element_type=jnp.float32
    ).astype(jnp.bfloat16)
    positions = projected.shape[1]
    tabs = make_tables()
    spectra = filter_spectra(filters.reshape(2, per, SIDE // 2, SIDE), tabs)
    grouped = jnp.swapaxes(projected.reshape(3, groups, per, positions), 0, 1)
    spread = lax.all_to_all(
        grouped.reshape(groups, 3 * per, positions), "seq", split_axis=0, concat_axis=0, tiled=True
    )
    spread = jnp.swapaxes(spread, 0, 1)
    me = lax.axis_index("seq")
    taps = lax.dynamic_slice_in_dim(short_w.reshape(9, groups, per), me, 1, axis=1)
    state = chain(
        spread.reshape(3, per, SIDE // 2, SIDE),
        spectra,
        filter_bias,
        taps.reshape(9, per),
        tabs,
    ).reshape(per, groups * positions)
    returned = lax.all_to_all(state, "seq", split_axis=1, concat_axis=0, tiled=True)
    output = lax.dot_general(
        returned, w_out, (((0,), (0,)), ((), ())), preferred_element_type=jnp.float32
    )
    return output.astype(jnp.bfloat16)


def solution(mesh):
    return jax.shard_map(
        local,
        mesh=mesh,
        in_specs=(P(("win", "seq"), None), P(), P(), P(None, "seq", None), P(None, "seq"), P()),
        out_specs=P(("win", "seq"), None),
        check_vma=False,
    )
```

```python
import math

import jax
import jax.numpy as jnp
from jax import lax
from jax.experimental import pallas as pl
from jax.experimental.pallas import tpu as pltpu
from jax.sharding import PartitionSpec as P

SIDE = 256


def halves(values):
    upper = values.astype(jnp.bfloat16)
    return upper, (values - upper.astype(jnp.float32)).astype(jnp.bfloat16)


def product(left, right):
    left_hi, left_lo = halves(left)
    right_hi, right_lo = halves(right)
    total = jnp.dot(left_hi, right_hi, preferred_element_type=jnp.float32)
    total = total + jnp.dot(left_lo, right_hi, preferred_element_type=jnp.float32)
    return total + jnp.dot(left_hi, right_lo, preferred_element_type=jnp.float32)


def single(left, right):
    return jnp.dot(
        left.astype(jnp.bfloat16), right.astype(jnp.bfloat16), preferred_element_type=jnp.float32
    )


def make_tables():
    rows = lax.broadcasted_iota(jnp.int32, (SIDE, SIDE), 0)
    cols = lax.broadcasted_iota(jnp.int32, (SIDE, SIDE), 1)
    rows, cols = lax.optimization_barrier((rows, cols))
    step = -2.0 * math.pi / SIDE
    small = ((rows * cols) % SIDE).astype(jnp.float32) * step
    big = (rows * cols).astype(jnp.float32) * (step / SIDE)
    f_re, f_im = jnp.cos(small), jnp.sin(small)
    half = SIDE // 2
    left_fwd = jnp.concatenate([f_re[:, :half], f_im[:, :half]], 0)
    right_fwd = jnp.concatenate(
        [jnp.concatenate([f_re, f_im], 1), jnp.concatenate([-f_im, f_re], 1)], 0
    )
    right_inv = jnp.concatenate(
        [jnp.concatenate([f_re, -f_im], 1), jnp.concatenate([f_im, f_re], 1)], 0
    )
    left_inv = jnp.concatenate([f_re[:half], f_im[:half]], 1)
    return left_fwd, right_fwd, right_inv, left_inv, jnp.cos(big), jnp.sin(big)


def spectrum(rows_in, left_fwd, right_fwd, tw_re, tw_im, mul):
    stacked = mul(left_fwd, rows_in)
    b_re, b_im = stacked[:SIDE], stacked[SIDE:]
    t_re = b_re * tw_re - b_im * tw_im
    t_im = b_re * tw_im + b_im * tw_re
    return mul(jnp.concatenate([t_re, t_im], 1), right_fwd)


def filter_kernel(filt_ref, lf_ref, rf_ref, twr_ref, twi_ref, out_ref):
    out_ref[0, 0] = spectrum(
        filt_ref[0, 0], lf_ref[...], rf_ref[...], twr_ref[...], twi_ref[...], product
    )


def filter_spectra(filters, tabs):
    left_fwd, right_fwd, _, _, tw_re, tw_im = tabs
    orders, per = filters.shape[:2]
    half = SIDE // 2
    full = lambda shape: pl.BlockSpec(shape, lambda o, c: (0,) * len(shape))
    return pl.pallas_call(
        filter_kernel,
        grid=(orders, per),
        in_specs=[
            pl.BlockSpec((1, 1, half, SIDE), lambda o, c: (o, c, 0, 0)),
            full((2 * SIDE, half)),
            full((2 * SIDE, 2 * SIDE)),
            full((SIDE, SIDE)),
            full((SIDE, SIDE)),
        ],
        out_specs=pl.BlockSpec((1, 1, SIDE, 2 * SIDE), lambda o, c: (o, c, 0, 0)),
        out_shape=jax.ShapeDtypeStruct((orders, per, SIDE, 2 * SIDE), jnp.float32),
        compiler_params=pltpu.CompilerParams(vmem_limit_bytes=48 * 1024 * 1024),
    )(filters, left_fwd, right_fwd, tw_re, tw_im)


def convolve(sig, f_spec, bias, tabs):
    left_fwd, right_fwd, right_inv, left_inv, tw_re, tw_im = tabs
    signal = sig.astype(jnp.float32)
    s_spec = spectrum(sig, left_fwd, right_fwd, tw_re, tw_im, single)
    s_re, s_im = s_spec[:, :SIDE], s_spec[:, SIDE:]
    f_re, f_im = f_spec[:, :SIDE], f_spec[:, SIDE:]
    p_re = s_re * f_re - s_im * f_im
    p_im = s_re * f_im + s_im * f_re
    d = single(jnp.concatenate([p_re, p_im], 1), right_inv)
    d_re, d_im = d[:, :SIDE], d[:, SIDE:]
    e_re = d_re * tw_re + d_im * tw_im
    e_im = d_im * tw_re - d_re * tw_im
    back = single(left_inv, jnp.concatenate([e_re, e_im], 0))
    scale = 1.0 / (SIDE * SIDE)
    return (back * scale + bias * signal).astype(jnp.bfloat16)


def chain_kernel(short_ref, spec_ref, bias_ref, lf_ref, rf_ref, ri_ref, li_ref, twr_ref, twi_ref, out_ref):
    channel = pl.program_id(0)
    tabs = (lf_ref[...], rf_ref[...], ri_ref[...], li_ref[...], twr_ref[...], twi_ref[...])
    state = short_ref[2, 0]
    for order in range(2):
        conv = convolve(state, spec_ref[order, 0], bias_ref[order, channel], tabs)
        state = (short_ref[order, 0].astype(jnp.float32) * conv.astype(jnp.float32)).astype(jnp.bfloat16)
    out_ref[0] = state


def chain(short, spectra, bias, tabs):
    per = short.shape[1]
    half = SIDE // 2
    left_fwd, right_fwd, right_inv, left_inv, tw_re, tw_im = tabs
    low = lambda t: t.astype(jnp.bfloat16)
    full = lambda shape: pl.BlockSpec(shape, lambda c: (0,) * len(shape))
    return pl.pallas_call(
        chain_kernel,
        grid=(per,),
        in_specs=[
            pl.BlockSpec((3, 1, half, SIDE), lambda c: (0, c, 0, 0)),
            pl.BlockSpec((2, 1, SIDE, 2 * SIDE), lambda c: (0, c, 0, 0)),
            pl.BlockSpec(memory_space=pltpu.SMEM),
            full((2 * SIDE, half)),
            full((2 * SIDE, 2 * SIDE)),
            full((2 * SIDE, 2 * SIDE)),
            full((half, 2 * SIDE)),
            full((SIDE, SIDE)),
            full((SIDE, SIDE)),
        ],
        out_specs=pl.BlockSpec((1, half, SIDE), lambda c: (c, 0, 0)),
        out_shape=jax.ShapeDtypeStruct((per, half, SIDE), jnp.bfloat16),
        compiler_params=pltpu.CompilerParams(vmem_limit_bytes=48 * 1024 * 1024),
    )(short, spectra, bias, low(left_fwd), low(right_fwd), low(right_inv), low(left_inv), tw_re, tw_im)


SEQ = ("g", "core")


def spread_out(grouped):
    chips, cores = lax.axis_size("g"), lax.axis_size("core")
    y = grouped.reshape((chips, cores) + grouped.shape[1:])
    first = lax.axis_index("core") == 0
    keep = jnp.where(first, y[:, 0], y[:, 1])
    give = jnp.where(first, y[:, 1], y[:, 0])
    got = lax.ppermute(give, "core", [(0, 1), (1, 0)])
    z = jnp.stack([jnp.where(first, keep, got), jnp.where(first, got, keep)], 1)
    z = lax.all_to_all(z, "g", split_axis=0, concat_axis=0, tiled=True)
    return z.reshape(grouped.shape)


def bring_back(state):
    chips, cores = lax.axis_size("g"), lax.axis_size("core")
    per, length = state.shape
    s = jnp.transpose(state.reshape(per, chips, cores, length // (chips * cores)), (1, 2, 0, 3))
    r = lax.all_to_all(s, "g", split_axis=0, concat_axis=0, tiled=True)
    first = lax.axis_index("core") == 0
    keep = jnp.where(first, r[:, 0], r[:, 1])
    give = jnp.where(first, r[:, 1], r[:, 0])
    got = lax.ppermute(give, "core", [(0, 1), (1, 0)])
    z = jnp.stack([jnp.where(first, keep, got), jnp.where(first, got, keep)], 1)
    return z.reshape(chips * cores * per, length // (chips * cores))


def local(layer_input, w_in, short_w, filters, filter_bias, w_out):
    width = w_out.shape[0]
    groups = lax.axis_size("g") * lax.axis_size("core")
    per = width // groups
    projected = lax.dot_general(
        w_in, layer_input, (((0,), (1,)), ((), ())), preferred_element_type=jnp.float32
    ).astype(jnp.bfloat16)
    positions = projected.shape[1]
    tabs = make_tables()
    spectra = filter_spectra(filters.reshape(2, per, SIDE // 2, SIDE), tabs)
    grouped = jnp.swapaxes(projected.reshape(3, groups, per, positions), 0, 1)
    spread = spread_out(grouped.reshape(groups, 3 * per, positions))
    spread = jnp.swapaxes(spread, 0, 1).reshape(3 * per, groups * positions)
    me = lax.axis_index("g") * lax.axis_size("core") + lax.axis_index("core")
    taps = lax.dynamic_slice_in_dim(short_w.reshape(3, 3, groups, per), me, 1, axis=2)
    taps = taps.reshape(3, 3 * per)
    extended = jnp.pad(spread.astype(jnp.float32), ((0, 0), (2, 0)))
    length = spread.shape[1]
    short = (
        taps[0][:, None] * extended[:, 2:]
        + taps[1][:, None] * extended[:, 1 : length + 1]
        + taps[2][:, None] * extended[:, :length]
    ).astype(jnp.bfloat16)
    half = SIDE // 2
    state = chain(
        short.reshape(3, per, half, SIDE),
        spectra,
        filter_bias,
        tabs,
    ).reshape(per, length)
    returned = bring_back(state)
    output = lax.dot_general(
        returned, w_out, (((0,), (0,)), ((), ())), preferred_element_type=jnp.float32
    )
    return output.astype(jnp.bfloat16)


def solution(mesh):
    wins, seqs = mesh.devices.shape
    view = jax.sharding.Mesh(mesh.devices.reshape(wins, seqs // 2, 2), ("win",) + SEQ)
    rows = ("win",) + SEQ
    return jax.shard_map(
        local,
        mesh=view,
        in_specs=(P(rows, None), P(), P(), P(None, SEQ, None), P(None, SEQ), P()),
        out_specs=P(rows, None),
        check_vma=False,
    )
```

```python
import functools
import math

import jax
import jax.numpy as jnp
from jax import lax
from jax.experimental import pallas as pl
from jax.experimental.pallas import tpu as pltpu
from jax.sharding import PartitionSpec as P

SIDE = 256


def halves(values):
    upper = values.astype(jnp.bfloat16)
    return upper, (values - upper.astype(jnp.float32)).astype(jnp.bfloat16)


def product(left, right):
    left_hi, left_lo = halves(left)
    right_hi, right_lo = halves(right)
    total = jnp.dot(left_hi, right_hi, preferred_element_type=jnp.float32)
    total = total + jnp.dot(left_lo, right_hi, preferred_element_type=jnp.float32)
    return total + jnp.dot(left_hi, right_lo, preferred_element_type=jnp.float32)


def single(left, right):
    return jnp.dot(
        left.astype(jnp.bfloat16), right.astype(jnp.bfloat16), preferred_element_type=jnp.float32
    )


def make_tables():
    rows = lax.broadcasted_iota(jnp.int32, (SIDE, SIDE), 0)
    cols = lax.broadcasted_iota(jnp.int32, (SIDE, SIDE), 1)
    rows, cols = lax.optimization_barrier((rows, cols))
    step = -2.0 * math.pi / SIDE
    small = ((rows * cols) % SIDE).astype(jnp.float32) * step
    big = (rows * cols).astype(jnp.float32) * (step / SIDE)
    f_re, f_im = jnp.cos(small), jnp.sin(small)
    half = SIDE // 2
    left_fwd = jnp.concatenate([f_re[:, :half], f_im[:, :half]], 0)
    right_fwd = jnp.concatenate(
        [jnp.concatenate([f_re, f_im], 1), jnp.concatenate([-f_im, f_re], 1)], 0
    )
    right_inv = jnp.concatenate(
        [jnp.concatenate([f_re, -f_im], 1), jnp.concatenate([f_im, f_re], 1)], 0
    )
    left_inv = jnp.concatenate([f_re[:half], f_im[:half]], 1)
    return left_fwd, right_fwd, right_inv, left_inv, jnp.cos(big), jnp.sin(big)


def spectrum(rows_in, left_fwd, right_fwd, tw_re, tw_im, mul):
    stacked = mul(left_fwd, rows_in)
    b_re, b_im = stacked[:SIDE], stacked[SIDE:]
    t_re = b_re * tw_re - b_im * tw_im
    t_im = b_re * tw_im + b_im * tw_re
    return mul(jnp.concatenate([t_re, t_im], 1), right_fwd)


def filter_kernel(filt_ref, lf_ref, rf_ref, twr_ref, twi_ref, out_ref):
    out_ref[0, 0] = spectrum(
        filt_ref[0, 0], lf_ref[...], rf_ref[...], twr_ref[...], twi_ref[...], product
    )


def filter_spectra(filters, tabs):
    left_fwd, right_fwd, _, _, tw_re, tw_im = tabs
    orders, per = filters.shape[:2]
    half = SIDE // 2
    full = lambda shape: pl.BlockSpec(shape, lambda o, c: (0,) * len(shape))
    return pl.pallas_call(
        filter_kernel,
        grid=(orders, per),
        in_specs=[
            pl.BlockSpec((1, 1, half, SIDE), lambda o, c: (o, c, 0, 0)),
            full((2 * SIDE, half)),
            full((2 * SIDE, 2 * SIDE)),
            full((SIDE, SIDE)),
            full((SIDE, SIDE)),
        ],
        out_specs=pl.BlockSpec((1, 1, SIDE, 2 * SIDE), lambda o, c: (o, c, 0, 0)),
        out_shape=jax.ShapeDtypeStruct((orders, per, SIDE, 2 * SIDE), jnp.float32),
        compiler_params=pltpu.CompilerParams(vmem_limit_bytes=48 * 1024 * 1024),
    )(filters, left_fwd, right_fwd, tw_re, tw_im)


def convolve(sig, f_spec, bias, tabs):
    left_fwd, right_fwd, right_inv, left_inv, tw_re, tw_im = tabs
    signal = sig.astype(jnp.float32)
    s_spec = spectrum(sig, left_fwd, right_fwd, tw_re, tw_im, single)
    s_re, s_im = s_spec[:, :SIDE], s_spec[:, SIDE:]
    f_re, f_im = f_spec[:, :SIDE], f_spec[:, SIDE:]
    p_re = s_re * f_re - s_im * f_im
    p_im = s_re * f_im + s_im * f_re
    d = single(jnp.concatenate([p_re, p_im], 1), right_inv)
    d_re, d_im = d[:, :SIDE], d[:, SIDE:]
    e_re = d_re * tw_re + d_im * tw_im
    e_im = d_im * tw_re - d_re * tw_im
    back = single(left_inv, jnp.concatenate([e_re, e_im], 0))
    scale = 1.0 / (SIDE * SIDE)
    return (back * scale + bias * signal).astype(jnp.bfloat16)


def chain_kernel(
    rows_ref, spec_ref, bias_ref, taps_ref,
    lf_ref, rf_ref, ri_ref, li_ref, twr_ref, twi_ref, out_ref, *, per,
):
    half = SIDE // 2
    tabs = (lf_ref[...], rf_ref[...], ri_ref[...], li_ref[...], twr_ref[...], twi_ref[...])
    big_r = lax.broadcasted_iota(jnp.int32, (2 * SIDE, 2 * SIDE), 0)
    big_c = lax.broadcasted_iota(jnp.int32, (2 * SIDE, 2 * SIDE), 1)
    origin = jnp.where(big_r < SIDE, big_r, big_r - 2 * SIDE)
    lag = jnp.where(big_c < SIDE, 1, 2)
    target = jnp.where(big_c < SIDE, big_c, big_c - SIDE)
    shifts = (origin + lag == target).astype(jnp.bfloat16)
    small_r = lax.broadcasted_iota(jnp.int32, (half, half), 0)
    small_c = lax.broadcasted_iota(jnp.int32, (half, half), 1)
    carry = (small_c + 1 == small_r).astype(jnp.bfloat16)
    for channel in range(per):
        streams = []
        for stream in range(3):
            p = rows_ref[:, stream * per + channel, :].reshape(half, SIDE)
            q = jnp.dot(carry, p, preferred_element_type=jnp.float32).astype(jnp.bfloat16)
            moved = jnp.dot(jnp.concatenate([p, q], 1), shifts, preferred_element_type=jnp.float32)
            short = (
                taps_ref[stream, channel] * p.astype(jnp.float32)
                + taps_ref[3 + stream, channel] * moved[:, :SIDE]
                + taps_ref[6 + stream, channel] * moved[:, SIDE:]
            )
            streams.append(short.astype(jnp.bfloat16))
        state = streams[2]
        for order in range(2):
            conv = convolve(state, spec_ref[order, channel], bias_ref[order, channel], tabs)
            state = (streams[order].astype(jnp.float32) * conv.astype(jnp.float32)).astype(jnp.bfloat16)
        out_ref[channel] = state


def chain(rows, spectra, bias, taps, tabs, per):
    half = SIDE // 2
    left_fwd, right_fwd, right_inv, left_inv, tw_re, tw_im = tabs
    low = lambda t: t.astype(jnp.bfloat16)
    vmem = pl.BlockSpec(memory_space=pltpu.VMEM)
    smem = pl.BlockSpec(memory_space=pltpu.SMEM)
    return pl.pallas_call(
        functools.partial(chain_kernel, per=per),
        in_specs=[vmem, vmem, smem, smem] + [vmem] * 6,
        out_specs=vmem,
        out_shape=jax.ShapeDtypeStruct((per, half, SIDE), jnp.bfloat16),
        compiler_params=pltpu.CompilerParams(vmem_limit_bytes=48 * 1024 * 1024),
    )(
        rows, spectra, bias, taps,
        low(left_fwd), low(right_fwd), low(right_inv), low(left_inv), tw_re, tw_im,
    )


def local(layer_input, w_in, short_w, filters, filter_bias, w_out):
    width = w_out.shape[0]
    groups = lax.axis_size("seq")
    per = width // groups
    projected = lax.dot_general(
        w_in, layer_input, (((0,), (1,)), ((), ())), preferred_element_type=jnp.float32
    ).astype(jnp.bfloat16)
    positions = projected.shape[1]
    tabs = make_tables()
    spectra = filter_spectra(filters.reshape(2, per, SIDE // 2, SIDE), tabs)
    grouped = jnp.swapaxes(projected.reshape(3, groups, per, positions), 0, 1)
    spread = lax.all_to_all(
        grouped.reshape(groups, 3 * per, positions), "seq", split_axis=0, concat_axis=0, tiled=True
    )
    me = lax.axis_index("seq")
    taps = lax.dynamic_slice_in_dim(short_w.reshape(9, groups, per), me, 1, axis=1)
    state = chain(spread, spectra, filter_bias, taps.reshape(9, per), tabs, per)
    state = state.reshape(per, groups * positions)
    returned = lax.all_to_all(state, "seq", split_axis=1, concat_axis=0, tiled=True)
    output = lax.dot_general(
        returned, w_out, (((0,), (0,)), ((), ())), preferred_element_type=jnp.float32
    )
    return output.astype(jnp.bfloat16)


def solution(mesh):
    return jax.shard_map(
        local,
        mesh=mesh,
        in_specs=(P(("win", "seq"), None), P(), P(), P(None, "seq", None), P(None, "seq"), P()),
        out_specs=P(("win", "seq"), None),
        check_vma=False,
    )
```

```python
import math

import jax
import jax.numpy as jnp
from jax import lax
from jax.experimental import pallas as pl
from jax.experimental.pallas import tpu as pltpu
from jax.sharding import PartitionSpec as P

SIDE = 256


def halves(values):
    upper = values.astype(jnp.bfloat16)
    return upper, (values - upper.astype(jnp.float32)).astype(jnp.bfloat16)


def product(left, right):
    left_hi, left_lo = halves(left)
    right_hi, right_lo = halves(right)
    total = jnp.dot(left_hi, right_hi, preferred_element_type=jnp.float32)
    total = total + jnp.dot(left_lo, right_hi, preferred_element_type=jnp.float32)
    return total + jnp.dot(left_hi, right_lo, preferred_element_type=jnp.float32)


def single(left, right):
    return jnp.dot(
        left.astype(jnp.bfloat16), right.astype(jnp.bfloat16), preferred_element_type=jnp.float32
    )


def make_tables():
    rows = lax.broadcasted_iota(jnp.int32, (SIDE, SIDE), 0)
    cols = lax.broadcasted_iota(jnp.int32, (SIDE, SIDE), 1)
    rows, cols = lax.optimization_barrier((rows, cols))
    step = -2.0 * math.pi / SIDE
    small = ((rows * cols) % SIDE).astype(jnp.float32) * step
    big = (rows * cols).astype(jnp.float32) * (step / SIDE)
    f_re, f_im = jnp.cos(small), jnp.sin(small)
    half = SIDE // 2
    left_fwd = jnp.concatenate([f_re[:, :half], f_im[:, :half]], 0)
    right_fwd = jnp.concatenate(
        [jnp.concatenate([f_re, f_im], 1), jnp.concatenate([-f_im, f_re], 1)], 0
    )
    right_inv = jnp.concatenate(
        [jnp.concatenate([f_re, -f_im], 1), jnp.concatenate([f_im, f_re], 1)], 0
    )
    left_inv = jnp.concatenate([f_re[:half], f_im[:half]], 1)
    return left_fwd, right_fwd, right_inv, left_inv, jnp.cos(big), jnp.sin(big)


def spectrum(rows_in, left_fwd, right_fwd, tw_re, tw_im, mul):
    stacked = mul(left_fwd, rows_in)
    b_re, b_im = stacked[:SIDE], stacked[SIDE:]
    t_re = b_re * tw_re - b_im * tw_im
    t_im = b_re * tw_im + b_im * tw_re
    return mul(jnp.concatenate([t_re, t_im], 1), right_fwd)


def filter_kernel(filt_ref, lf_ref, rf_ref, twr_ref, twi_ref, out_ref):
    out_ref[0, 0] = spectrum(
        filt_ref[0, 0], lf_ref[...], rf_ref[...], twr_ref[...], twi_ref[...], product
    )


def filter_spectra(filters, tabs):
    left_fwd, right_fwd, _, _, tw_re, tw_im = tabs
    orders, per = filters.shape[:2]
    half = SIDE // 2
    full = lambda shape: pl.BlockSpec(shape, lambda o, c: (0,) * len(shape))
    return pl.pallas_call(
        filter_kernel,
        grid=(orders, per),
        in_specs=[
            pl.BlockSpec((1, 1, half, SIDE), lambda o, c: (o, c, 0, 0)),
            full((2 * SIDE, half)),
            full((2 * SIDE, 2 * SIDE)),
            full((SIDE, SIDE)),
            full((SIDE, SIDE)),
        ],
        out_specs=pl.BlockSpec((1, 1, SIDE, 2 * SIDE), lambda o, c: (o, c, 0, 0)),
        out_shape=jax.ShapeDtypeStruct((orders, per, SIDE, 2 * SIDE), jnp.float32),
        compiler_params=pltpu.CompilerParams(vmem_limit_bytes=48 * 1024 * 1024),
    )(filters, left_fwd, right_fwd, tw_re, tw_im)


def convolve(sig, f_spec, bias, tabs):
    left_fwd, right_fwd, right_inv, left_inv, tw_re, tw_im = tabs
    signal = sig.astype(jnp.float32)
    s_spec = spectrum(sig, left_fwd, right_fwd, tw_re, tw_im, single)
    s_re, s_im = s_spec[:, :SIDE], s_spec[:, SIDE:]
    f_re, f_im = f_spec[:, :SIDE], f_spec[:, SIDE:]
    p_re = s_re * f_re - s_im * f_im
    p_im = s_re * f_im + s_im * f_re
    d = single(jnp.concatenate([p_re, p_im], 1), right_inv)
    d_re, d_im = d[:, :SIDE], d[:, SIDE:]
    e_re = d_re * tw_re + d_im * tw_im
    e_im = d_im * tw_re - d_re * tw_im
    back = single(left_inv, jnp.concatenate([e_re, e_im], 0))
    scale = 1.0 / (SIDE * SIDE)
    return (back * scale + bias * signal).astype(jnp.bfloat16)


def chain_kernel(short_ref, spec_ref, bias_ref, lf_ref, rf_ref, ri_ref, li_ref, twr_ref, twi_ref, out_ref):
    channel = pl.program_id(0)
    tabs = (lf_ref[...], rf_ref[...], ri_ref[...], li_ref[...], twr_ref[...], twi_ref[...])
    state = short_ref[2, 0]
    for order in range(2):
        conv = convolve(state, spec_ref[order, 0], bias_ref[order, channel], tabs)
        state = (short_ref[order, 0].astype(jnp.float32) * conv.astype(jnp.float32)).astype(jnp.bfloat16)
    out_ref[0] = state


def chain(short, spectra, bias, tabs):
    per = short.shape[1]
    half = SIDE // 2
    left_fwd, right_fwd, right_inv, left_inv, tw_re, tw_im = tabs
    low = lambda t: t.astype(jnp.bfloat16)
    full = lambda shape: pl.BlockSpec(shape, lambda c: (0,) * len(shape))
    return pl.pallas_call(
        chain_kernel,
        grid=(per,),
        in_specs=[
            pl.BlockSpec((3, 1, half, SIDE), lambda c: (0, c, 0, 0)),
            pl.BlockSpec((2, 1, SIDE, 2 * SIDE), lambda c: (0, c, 0, 0)),
            pl.BlockSpec(memory_space=pltpu.SMEM),
            full((2 * SIDE, half)),
            full((2 * SIDE, 2 * SIDE)),
            full((2 * SIDE, 2 * SIDE)),
            full((half, 2 * SIDE)),
            full((SIDE, SIDE)),
            full((SIDE, SIDE)),
        ],
        out_specs=pl.BlockSpec((1, half, SIDE), lambda c: (c, 0, 0)),
        out_shape=jax.ShapeDtypeStruct((per, half, SIDE), jnp.bfloat16),
        compiler_params=pltpu.CompilerParams(vmem_limit_bytes=48 * 1024 * 1024),
    )(short, spectra, bias, low(left_fwd), low(right_fwd), low(right_inv), low(left_inv), tw_re, tw_im)


def local(layer_input, w_in, short_w, filters, filter_bias, w_out):
    width = w_out.shape[0]
    groups = lax.axis_size("seq")
    per = width // groups
    projected = lax.dot_general(
        w_in, layer_input, (((0,), (1,)), ((), ())), preferred_element_type=jnp.float32
    ).astype(jnp.bfloat16)
    positions = projected.shape[1]
    grouped = jnp.swapaxes(projected.reshape(3, groups, per, positions), 0, 1)
    tabs = make_tables()
    spectra = filter_spectra(filters.reshape(2, per, SIDE // 2, SIDE), tabs)
    spread = lax.all_to_all(grouped, "seq", split_axis=0, concat_axis=0, tiled=True)
    me = lax.axis_index("seq")
    taps = lax.dynamic_slice_in_dim(short_w.reshape(3, 3, groups, per), me, 1, axis=2)
    taps = taps.reshape(3, 1, 3, per, 1)
    signal = spread.astype(jnp.float32)
    edge = jnp.zeros((1, 3, per, 2), jnp.float32)
    before = jnp.concatenate([edge, signal[:-1, :, :, -2:]], 0)
    back_one = jnp.concatenate([before[:, :, :, 1:], signal[:, :, :, :-1]], 3)
    back_two = jnp.concatenate([before, signal[:, :, :, :-2]], 3)
    short = (taps[0] * signal + taps[1] * back_one + taps[2] * back_two).astype(jnp.bfloat16)
    length = groups * positions
    short = jnp.transpose(short, (1, 2, 0, 3))
    half = SIDE // 2
    state = chain(
        short.reshape(3, per, half, SIDE),
        spectra,
        filter_bias,
        tabs,
    ).reshape(per, length)
    returned = lax.all_to_all(state, "seq", split_axis=1, concat_axis=0, tiled=True)
    output = lax.dot_general(
        returned, w_out, (((0,), (0,)), ((), ())), preferred_element_type=jnp.float32
    )
    return output.astype(jnp.bfloat16)


def solution(mesh):
    return jax.shard_map(
        local,
        mesh=mesh,
        in_specs=(P(("win", "seq"), None), P(), P(), P(None, "seq", None), P(None, "seq"), P()),
        out_specs=P(("win", "seq"), None),
        check_vma=False,
    )
```

```python
import math

import jax
import jax.numpy as jnp
from jax import lax
from jax.experimental import pallas as pl
from jax.experimental.pallas import tpu as pltpu
from jax.sharding import PartitionSpec as P

SIDE = 256


def halves(values):
    upper = values.astype(jnp.bfloat16)
    return upper, (values - upper.astype(jnp.float32)).astype(jnp.bfloat16)


def product(left, right):
    left_hi, left_lo = halves(left)
    right_hi, right_lo = halves(right)
    total = jnp.dot(left_hi, right_hi, preferred_element_type=jnp.float32)
    total = total + jnp.dot(left_lo, right_hi, preferred_element_type=jnp.float32)
    return total + jnp.dot(left_hi, right_lo, preferred_element_type=jnp.float32)


def single(left, right):
    return jnp.dot(
        left.astype(jnp.bfloat16), right.astype(jnp.bfloat16), preferred_element_type=jnp.float32
    )


def make_tables():
    rows = lax.broadcasted_iota(jnp.int32, (SIDE, SIDE), 0)
    cols = lax.broadcasted_iota(jnp.int32, (SIDE, SIDE), 1)
    rows, cols = lax.optimization_barrier((rows, cols))
    step = -2.0 * math.pi / SIDE
    small = ((rows * cols) % SIDE).astype(jnp.float32) * step
    big = (rows * cols).astype(jnp.float32) * (step / SIDE)
    f_re, f_im = jnp.cos(small), jnp.sin(small)
    half = SIDE // 2
    left_fwd = jnp.concatenate([f_re[:, :half], f_im[:, :half]], 0)
    right_fwd = jnp.concatenate(
        [jnp.concatenate([f_re, f_im], 1), jnp.concatenate([-f_im, f_re], 1)], 0
    )
    right_inv = jnp.concatenate(
        [jnp.concatenate([f_re, -f_im], 1), jnp.concatenate([f_im, f_re], 1)], 0
    )
    left_inv = jnp.concatenate([f_re[:half], f_im[:half]], 1)
    return left_fwd, right_fwd, right_inv, left_inv, jnp.cos(big), jnp.sin(big), f_re, f_im


def spectrum(rows_in, left_fwd, right_fwd, tw_re, tw_im, mul):
    stacked = mul(left_fwd, rows_in)
    b_re, b_im = stacked[:SIDE], stacked[SIDE:]
    t_re = b_re * tw_re - b_im * tw_im
    t_im = b_re * tw_im + b_im * tw_re
    return mul(jnp.concatenate([t_re, t_im], 1), right_fwd)


def filter_kernel(filt_ref, lf_ref, rf_ref, twr_ref, twi_ref, out_ref):
    out_ref[0, 0] = spectrum(
        filt_ref[0, 0], lf_ref[...], rf_ref[...], twr_ref[...], twi_ref[...], product
    )


def filter_spectra(filters, tabs):
    left_fwd, right_fwd, _, _, tw_re, tw_im = tabs[:6]
    orders, per = filters.shape[:2]
    half = SIDE // 2
    full = lambda shape: pl.BlockSpec(shape, lambda o, c: (0,) * len(shape))
    return pl.pallas_call(
        filter_kernel,
        grid=(orders, per),
        in_specs=[
            pl.BlockSpec((1, 1, half, SIDE), lambda o, c: (o, c, 0, 0)),
            full((2 * SIDE, half)),
            full((2 * SIDE, 2 * SIDE)),
            full((SIDE, SIDE)),
            full((SIDE, SIDE)),
        ],
        out_specs=pl.BlockSpec((1, 1, SIDE, 2 * SIDE), lambda o, c: (o, c, 0, 0)),
        out_shape=jax.ShapeDtypeStruct((orders, per, SIDE, 2 * SIDE), jnp.float32),
        compiler_params=pltpu.CompilerParams(vmem_limit_bytes=48 * 1024 * 1024),
    )(filters, left_fwd, right_fwd, tw_re, tw_im)


def convolve(sig, f_spec, bias, tabs):
    left_fwd, right_fwd, right_inv, left_inv, tw_re, tw_im = tabs
    signal = sig.astype(jnp.float32)
    s_spec = spectrum(sig, left_fwd, right_fwd, tw_re, tw_im, single)
    s_re, s_im = s_spec[:, :SIDE], s_spec[:, SIDE:]
    f_re, f_im = f_spec[:, :SIDE], f_spec[:, SIDE:]
    p_re = s_re * f_re - s_im * f_im
    p_im = s_re * f_im + s_im * f_re
    d = single(jnp.concatenate([p_re, p_im], 1), right_inv)
    d_re, d_im = d[:, :SIDE], d[:, SIDE:]
    e_re = d_re * tw_re + d_im * tw_im
    e_im = d_im * tw_re - d_re * tw_im
    back = single(left_inv, jnp.concatenate([e_re, e_im], 0))
    scale = 1.0 / (SIDE * SIDE)
    return (back * scale + bias * signal).astype(jnp.bfloat16)


def chain_kernel(short_ref, spec_ref, bias_ref, fr_ref, fi_ref, twr_ref, twi_ref, out_ref):
    channel = pl.program_id(0)
    half = SIDE // 2
    f_re, f_im = fr_ref[...], fi_ref[...]
    left_fwd = jnp.concatenate([f_re[:, :half], f_im[:, :half]], 0)
    right_fwd = jnp.concatenate(
        [jnp.concatenate([f_re, f_im], 1), jnp.concatenate([-f_im, f_re], 1)], 0
    )
    right_inv = jnp.concatenate(
        [jnp.concatenate([f_re, -f_im], 1), jnp.concatenate([f_im, f_re], 1)], 0
    )
    left_inv = jnp.concatenate([f_re[:half], f_im[:half]], 1)
    tabs = (left_fwd, right_fwd, right_inv, left_inv, twr_ref[...], twi_ref[...])
    state = short_ref[2, 0]
    for order in range(2):
        conv = convolve(state, spec_ref[order, 0], bias_ref[order, channel], tabs)
        state = (short_ref[order, 0].astype(jnp.float32) * conv.astype(jnp.float32)).astype(jnp.bfloat16)
    out_ref[0] = state


def chain(short, spectra, bias, tabs):
    per = short.shape[1]
    half = SIDE // 2
    tw_re, tw_im, f_re, f_im = tabs[4:]
    full = lambda shape: pl.BlockSpec(shape, lambda c: (0,) * len(shape))
    return pl.pallas_call(
        chain_kernel,
        grid=(per,),
        in_specs=[
            pl.BlockSpec((3, 1, half, SIDE), lambda c: (0, c, 0, 0)),
            pl.BlockSpec((2, 1, SIDE, 2 * SIDE), lambda c: (0, c, 0, 0)),
            pl.BlockSpec(memory_space=pltpu.SMEM),
            full((SIDE, SIDE)),
            full((SIDE, SIDE)),
            full((SIDE, SIDE)),
            full((SIDE, SIDE)),
        ],
        out_specs=pl.BlockSpec((1, half, SIDE), lambda c: (c, 0, 0)),
        out_shape=jax.ShapeDtypeStruct((per, half, SIDE), jnp.bfloat16),
        compiler_params=pltpu.CompilerParams(vmem_limit_bytes=48 * 1024 * 1024),
    )(short, spectra, bias, f_re.astype(jnp.bfloat16), f_im.astype(jnp.bfloat16), tw_re, tw_im)


def local(layer_input, w_in, short_w, filters, filter_bias, w_out):
    width = w_out.shape[0]
    groups = lax.axis_size("seq")
    per = width // groups
    projected = lax.dot_general(
        w_in, layer_input, (((0,), (1,)), ((), ())), preferred_element_type=jnp.float32
    ).astype(jnp.bfloat16)
    positions = projected.shape[1]
    grouped = jnp.swapaxes(projected.reshape(3, groups, per, positions), 0, 1)
    tabs = make_tables()
    spectra = filter_spectra(filters.reshape(2, per, SIDE // 2, SIDE), tabs)
    spread = lax.all_to_all(
        grouped.reshape(groups, 3 * per, positions), "seq", split_axis=0, concat_axis=2, tiled=True
    ).reshape(3 * per, groups * positions)
    me = lax.axis_index("seq")
    taps = lax.dynamic_slice_in_dim(short_w.reshape(3, 3, groups, per), me, 1, axis=2)
    taps = taps.reshape(3, 3 * per)
    extended = jnp.pad(spread.astype(jnp.float32), ((0, 0), (2, 0)))
    length = spread.shape[1]
    short = (
        taps[0][:, None] * extended[:, 2:]
        + taps[1][:, None] * extended[:, 1 : length + 1]
        + taps[2][:, None] * extended[:, :length]
    ).astype(jnp.bfloat16)
    half = SIDE // 2
    state = chain(
        short.reshape(3, per, half, SIDE),
        spectra,
        filter_bias,
        tabs,
    ).reshape(per, length)
    returned = lax.all_to_all(state, "seq", split_axis=1, concat_axis=0, tiled=True)
    output = lax.dot_general(
        returned, w_out, (((0,), (0,)), ((), ())), preferred_element_type=jnp.float32
    )
    return output.astype(jnp.bfloat16)


def solution(mesh):
    return jax.shard_map(
        local,
        mesh=mesh,
        in_specs=(P(("win", "seq"), None), P(), P(), P(None, "seq", None), P(None, "seq"), P()),
        out_specs=P(("win", "seq"), None),
        check_vma=False,
    )
```

```python
import math

import jax
import jax.numpy as jnp
from jax import lax
from jax.experimental import pallas as pl
from jax.experimental.pallas import tpu as pltpu
from jax.sharding import PartitionSpec as P

SIDE = 256


def halves(values):
    upper = values.astype(jnp.bfloat16)
    return upper, (values - upper.astype(jnp.float32)).astype(jnp.bfloat16)


def product(left, right):
    left_hi, left_lo = halves(left)
    right_hi, right_lo = halves(right)
    total = jnp.dot(left_hi, right_hi, preferred_element_type=jnp.float32)
    total = total + jnp.dot(left_lo, right_hi, preferred_element_type=jnp.float32)
    return total + jnp.dot(left_hi, right_lo, preferred_element_type=jnp.float32)


def single(left, right):
    return jnp.dot(
        left.astype(jnp.bfloat16), right.astype(jnp.bfloat16), preferred_element_type=jnp.float32
    )


def make_tables():
    rows = lax.broadcasted_iota(jnp.int32, (SIDE, SIDE), 0)
    cols = lax.broadcasted_iota(jnp.int32, (SIDE, SIDE), 1)
    rows, cols = lax.optimization_barrier((rows, cols))
    step = -2.0 * math.pi / SIDE
    small = ((rows * cols) % SIDE).astype(jnp.float32) * step
    big = (rows * cols).astype(jnp.float32) * (step / SIDE)
    f_re, f_im = jnp.cos(small), jnp.sin(small)
    half = SIDE // 2
    left_fwd = jnp.concatenate([f_re[:, :half], f_im[:, :half]], 0)
    right_fwd = jnp.concatenate(
        [jnp.concatenate([f_re, f_im], 1), jnp.concatenate([-f_im, f_re], 1)], 0
    )
    right_inv = jnp.concatenate(
        [jnp.concatenate([f_re, -f_im], 1), jnp.concatenate([f_im, f_re], 1)], 0
    )
    left_inv = jnp.concatenate([f_re[:half], f_im[:half]], 1)
    return left_fwd, right_fwd, right_inv, left_inv, jnp.cos(big), jnp.sin(big), f_re, f_im


def spectrum(rows_in, left_fwd, right_fwd, tw_re, tw_im, mul):
    stacked = mul(left_fwd, rows_in)
    b_re, b_im = stacked[:SIDE], stacked[SIDE:]
    t_re = b_re * tw_re - b_im * tw_im
    t_im = b_re * tw_im + b_im * tw_re
    return mul(jnp.concatenate([t_re, t_im], 1), right_fwd)


def filter_kernel(filt_ref, fr_ref, fi_ref, twr_ref, twi_ref, out_ref):
    half = SIDE // 2
    f_re, f_im = fr_ref[...], fi_ref[...]
    left_fwd = jnp.concatenate([f_re[:, :half], f_im[:, :half]], 0)
    right_fwd = jnp.concatenate(
        [jnp.concatenate([f_re, f_im], 1), jnp.concatenate([-f_im, f_re], 1)], 0
    )
    out_ref[0, 0] = spectrum(
        filt_ref[0, 0], left_fwd, right_fwd, twr_ref[...], twi_ref[...], product
    )


def filter_spectra(filters, tabs):
    tw_re, tw_im, f_re, f_im = tabs[4:]
    orders, per = filters.shape[:2]
    half = SIDE // 2
    full = lambda shape: pl.BlockSpec(shape, lambda o, c: (0,) * len(shape))
    return pl.pallas_call(
        filter_kernel,
        grid=(orders, per),
        in_specs=[
            pl.BlockSpec((1, 1, half, SIDE), lambda o, c: (o, c, 0, 0)),
            full((SIDE, SIDE)),
            full((SIDE, SIDE)),
            full((SIDE, SIDE)),
            full((SIDE, SIDE)),
        ],
        out_specs=pl.BlockSpec((1, 1, SIDE, 2 * SIDE), lambda o, c: (o, c, 0, 0)),
        out_shape=jax.ShapeDtypeStruct((orders, per, SIDE, 2 * SIDE), jnp.float32),
        compiler_params=pltpu.CompilerParams(vmem_limit_bytes=48 * 1024 * 1024),
    )(filters, f_re, f_im, tw_re, tw_im)


def convolve(sig, f_spec, bias, tabs):
    left_fwd, right_fwd, right_inv, left_inv, tw_re, tw_im = tabs
    signal = sig.astype(jnp.float32)
    s_spec = spectrum(sig, left_fwd, right_fwd, tw_re, tw_im, single)
    s_re, s_im = s_spec[:, :SIDE], s_spec[:, SIDE:]
    f_re, f_im = f_spec[:, :SIDE], f_spec[:, SIDE:]
    p_re = s_re * f_re - s_im * f_im
    p_im = s_re * f_im + s_im * f_re
    d = single(jnp.concatenate([p_re, p_im], 1), right_inv)
    d_re, d_im = d[:, :SIDE], d[:, SIDE:]
    e_re = d_re * tw_re + d_im * tw_im
    e_im = d_im * tw_re - d_re * tw_im
    back = single(left_inv, jnp.concatenate([e_re, e_im], 0))
    scale = 1.0 / (SIDE * SIDE)
    return (back * scale + bias * signal).astype(jnp.bfloat16)


def chain_kernel(short_ref, spec_ref, bias_ref, fr_ref, fi_ref, twr_ref, twi_ref, out_ref):
    channel = pl.program_id(0)
    half = SIDE // 2
    f_re, f_im = fr_ref[...], fi_ref[...]
    left_fwd = jnp.concatenate([f_re[:, :half], f_im[:, :half]], 0)
    right_fwd = jnp.concatenate(
        [jnp.concatenate([f_re, f_im], 1), jnp.concatenate([-f_im, f_re], 1)], 0
    )
    right_inv = jnp.concatenate(
        [jnp.concatenate([f_re, -f_im], 1), jnp.concatenate([f_im, f_re], 1)], 0
    )
    left_inv = jnp.concatenate([f_re[:half], f_im[:half]], 1)
    tabs = (left_fwd, right_fwd, right_inv, left_inv, twr_ref[...], twi_ref[...])
    state = short_ref[2, 0]
    for order in range(2):
        conv = convolve(state, spec_ref[order, 0], bias_ref[order, channel], tabs)
        state = (short_ref[order, 0].astype(jnp.float32) * conv.astype(jnp.float32)).astype(jnp.bfloat16)
    out_ref[0] = state


def chain(short, spectra, bias, tabs):
    per = short.shape[1]
    half = SIDE // 2
    tw_re, tw_im, f_re, f_im = tabs[4:]
    full = lambda shape: pl.BlockSpec(shape, lambda c: (0,) * len(shape))
    return pl.pallas_call(
        chain_kernel,
        grid=(per,),
        in_specs=[
            pl.BlockSpec((3, 1, half, SIDE), lambda c: (0, c, 0, 0)),
            pl.BlockSpec((2, 1, SIDE, 2 * SIDE), lambda c: (0, c, 0, 0)),
            pl.BlockSpec(memory_space=pltpu.SMEM),
            full((SIDE, SIDE)),
            full((SIDE, SIDE)),
            full((SIDE, SIDE)),
            full((SIDE, SIDE)),
        ],
        out_specs=pl.BlockSpec((1, half, SIDE), lambda c: (c, 0, 0)),
        out_shape=jax.ShapeDtypeStruct((per, half, SIDE), jnp.bfloat16),
        compiler_params=pltpu.CompilerParams(vmem_limit_bytes=48 * 1024 * 1024),
    )(short, spectra, bias, f_re.astype(jnp.bfloat16), f_im.astype(jnp.bfloat16), tw_re, tw_im)


def local(layer_input, w_in, short_w, filters, filter_bias, w_out):
    width = w_out.shape[0]
    groups = lax.axis_size("seq")
    per = width // groups
    projected = lax.dot_general(
        w_in, layer_input, (((0,), (1,)), ((), ())), preferred_element_type=jnp.float32
    ).astype(jnp.bfloat16)
    positions = projected.shape[1]
    grouped = jnp.swapaxes(projected.reshape(3, groups, per, positions), 0, 1)
    tabs = make_tables()
    spectra = filter_spectra(filters.reshape(2, per, SIDE // 2, SIDE), tabs)
    spread = lax.all_to_all(
        grouped.reshape(groups, 3 * per, positions), "seq", split_axis=0, concat_axis=2, tiled=True
    ).reshape(3 * per, groups * positions)
    me = lax.axis_index("seq")
    taps = lax.dynamic_slice_in_dim(short_w.reshape(3, 3, groups, per), me, 1, axis=2)
    taps = taps.reshape(3, 3 * per)
    extended = jnp.pad(spread.astype(jnp.float32), ((0, 0), (2, 0)))
    length = spread.shape[1]
    short = (
        taps[0][:, None] * extended[:, 2:]
        + taps[1][:, None] * extended[:, 1 : length + 1]
        + taps[2][:, None] * extended[:, :length]
    ).astype(jnp.bfloat16)
    half = SIDE // 2
    state = chain(
        short.reshape(3, per, half, SIDE),
        spectra,
        filter_bias,
        tabs,
    ).reshape(per, length)
    returned = lax.all_to_all(state, "seq", split_axis=1, concat_axis=0, tiled=True)
    output = lax.dot_general(
        returned, w_out, (((0,), (0,)), ((), ())), preferred_element_type=jnp.float32
    )
    return output.astype(jnp.bfloat16)


def solution(mesh):
    return jax.shard_map(
        local,
        mesh=mesh,
        in_specs=(P(("win", "seq"), None), P(), P(), P(None, "seq", None), P(None, "seq"), P()),
        out_specs=P(("win", "seq"), None),
        check_vma=False,
    )
```

```python
import math

import jax
import jax.numpy as jnp
from jax import lax
from jax.experimental import pallas as pl
from jax.experimental.pallas import tpu as pltpu
from jax.sharding import PartitionSpec as P

SIDE = 256


def halves(values):
    upper = values.astype(jnp.bfloat16)
    return upper, (values - upper.astype(jnp.float32)).astype(jnp.bfloat16)


def product(left, right):
    left_hi, left_lo = halves(left)
    right_hi, right_lo = halves(right)
    total = jnp.dot(left_hi, right_hi, preferred_element_type=jnp.float32)
    total = total + jnp.dot(left_lo, right_hi, preferred_element_type=jnp.float32)
    return total + jnp.dot(left_hi, right_lo, preferred_element_type=jnp.float32)


def single(left, right):
    return jnp.dot(
        left.astype(jnp.bfloat16), right.astype(jnp.bfloat16), preferred_element_type=jnp.float32
    )


def make_tables():
    rows = lax.broadcasted_iota(jnp.int32, (SIDE, SIDE), 0)
    cols = lax.broadcasted_iota(jnp.int32, (SIDE, SIDE), 1)
    rows, cols = lax.optimization_barrier((rows, cols))
    step = -2.0 * math.pi / SIDE
    small = ((rows * cols) % SIDE).astype(jnp.float32) * step
    big = (rows * cols).astype(jnp.float32) * (step / SIDE)
    f_re, f_im = jnp.cos(small), jnp.sin(small)
    half = SIDE // 2
    left_fwd = jnp.concatenate([f_re[:, :half], f_im[:, :half]], 0)
    right_fwd = jnp.concatenate(
        [jnp.concatenate([f_re, f_im], 1), jnp.concatenate([-f_im, f_re], 1)], 0
    )
    right_inv = jnp.concatenate(
        [jnp.concatenate([f_re, -f_im], 1), jnp.concatenate([f_im, f_re], 1)], 0
    )
    left_inv = jnp.concatenate([f_re[:half], f_im[:half]], 1)
    return left_fwd, right_fwd, right_inv, left_inv, jnp.cos(big), jnp.sin(big), f_re, f_im


def spectrum(rows_in, left_fwd, right_fwd, tw_re, tw_im, mul):
    stacked = mul(left_fwd, rows_in)
    b_re, b_im = stacked[:SIDE], stacked[SIDE:]
    t_re = b_re * tw_re - b_im * tw_im
    t_im = b_re * tw_im + b_im * tw_re
    return mul(jnp.concatenate([t_re, t_im], 1), right_fwd)


def filter_kernel(filt_ref, lf_ref, rf_ref, twr_ref, twi_ref, out_ref):
    out_ref[0, 0] = spectrum(
        filt_ref[0, 0], lf_ref[...], rf_ref[...], twr_ref[...], twi_ref[...], product
    )


def filter_spectra(filters, tabs):
    left_fwd, right_fwd, _, _, tw_re, tw_im = tabs[:6]
    orders, per = filters.shape[:2]
    half = SIDE // 2
    full = lambda shape: pl.BlockSpec(shape, lambda o, c: (0,) * len(shape))
    return pl.pallas_call(
        filter_kernel,
        grid=(orders, per),
        in_specs=[
            pl.BlockSpec((1, 1, half, SIDE), lambda o, c: (o, c, 0, 0)),
            full((2 * SIDE, half)),
            full((2 * SIDE, 2 * SIDE)),
            full((SIDE, SIDE)),
            full((SIDE, SIDE)),
        ],
        out_specs=pl.BlockSpec((1, 1, SIDE, 2 * SIDE), lambda o, c: (o, c, 0, 0)),
        out_shape=jax.ShapeDtypeStruct((orders, per, SIDE, 2 * SIDE), jnp.float32),
        compiler_params=pltpu.CompilerParams(vmem_limit_bytes=48 * 1024 * 1024),
    )(filters, left_fwd, right_fwd, tw_re, tw_im)


def convolve(sig, f_spec, bias, tabs):
    left_fwd, right_fwd, right_inv, left_inv, tw_re, tw_im = tabs
    signal = sig.astype(jnp.float32)
    s_spec = spectrum(sig, left_fwd, right_fwd, tw_re, tw_im, single)
    s_re, s_im = s_spec[:, :SIDE], s_spec[:, SIDE:]
    f_re, f_im = f_spec[:, :SIDE], f_spec[:, SIDE:]
    p_re = s_re * f_re - s_im * f_im
    p_im = s_re * f_im + s_im * f_re
    d = single(jnp.concatenate([p_re, p_im], 1), right_inv)
    d_re, d_im = d[:, :SIDE], d[:, SIDE:]
    e_re = d_re * tw_re + d_im * tw_im
    e_im = d_im * tw_re - d_re * tw_im
    back = single(left_inv, jnp.concatenate([e_re, e_im], 0))
    scale = 1.0 / (SIDE * SIDE)
    return (back * scale + bias * signal).astype(jnp.bfloat16)


def chain_kernel(short_ref, spec_ref, bias_ref, fr_ref, fi_ref, twr_ref, twi_ref, out_ref):
    channel = pl.program_id(0)
    half = SIDE // 2
    f_re, f_im = fr_ref[...], fi_ref[...]
    left_fwd = jnp.concatenate([f_re[:, :half], f_im[:, :half]], 0)
    right_fwd = jnp.concatenate(
        [jnp.concatenate([f_re, f_im], 1), jnp.concatenate([-f_im, f_re], 1)], 0
    )
    right_inv = jnp.concatenate(
        [jnp.concatenate([f_re, -f_im], 1), jnp.concatenate([f_im, f_re], 1)], 0
    )
    left_inv = jnp.concatenate([f_re[:half], f_im[:half]], 1)
    tabs = (left_fwd, right_fwd, right_inv, left_inv, twr_ref[...], twi_ref[...])
    state = short_ref[2, 0]
    for order in range(2):
        conv = convolve(state, spec_ref[order, 0], bias_ref[order, channel], tabs)
        state = (short_ref[order, 0].astype(jnp.float32) * conv.astype(jnp.float32)).astype(jnp.bfloat16)
    out_ref[0] = state


def chain(short, spectra, bias, tabs):
    per = short.shape[1]
    half = SIDE // 2
    tw_re, tw_im, f_re, f_im = tabs[4:]
    full = lambda shape: pl.BlockSpec(shape, lambda c: (0,) * len(shape))
    return pl.pallas_call(
        chain_kernel,
        grid=(per,),
        in_specs=[
            pl.BlockSpec((3, 1, half, SIDE), lambda c: (0, c, 0, 0)),
            pl.BlockSpec((2, 1, SIDE, 2 * SIDE), lambda c: (0, c, 0, 0)),
            pl.BlockSpec(memory_space=pltpu.SMEM),
            full((SIDE, SIDE)),
            full((SIDE, SIDE)),
            full((SIDE, SIDE)),
            full((SIDE, SIDE)),
        ],
        out_specs=pl.BlockSpec((1, half, SIDE), lambda c: (c, 0, 0)),
        out_shape=jax.ShapeDtypeStruct((per, half, SIDE), jnp.bfloat16),
        compiler_params=pltpu.CompilerParams(vmem_limit_bytes=48 * 1024 * 1024),
    )(short, spectra, bias, f_re.astype(jnp.bfloat16), f_im.astype(jnp.bfloat16), tw_re, tw_im)


def out_kernel(rows_ref, w_ref, out_ref):
    rows = jnp.transpose(rows_ref[...].astype(jnp.float32)).astype(jnp.bfloat16)
    out_ref[...] = jnp.dot(rows, w_ref[...], preferred_element_type=jnp.float32).astype(jnp.bfloat16)


def local(layer_input, w_in, short_w, filters, filter_bias, w_out):
    width = w_out.shape[0]
    groups = lax.axis_size("seq")
    per = width // groups
    projected = lax.dot_general(
        w_in, layer_input, (((0,), (1,)), ((), ())), preferred_element_type=jnp.float32
    ).astype(jnp.bfloat16)
    positions = projected.shape[1]
    grouped = jnp.swapaxes(projected.reshape(3, groups, per, positions), 0, 1)
    tabs = make_tables()
    spectra = filter_spectra(filters.reshape(2, per, SIDE // 2, SIDE), tabs)
    spread = lax.all_to_all(
        grouped.reshape(groups, 3 * per, positions), "seq", split_axis=0, concat_axis=2, tiled=True
    ).reshape(3 * per, groups * positions)
    me = lax.axis_index("seq")
    taps = lax.dynamic_slice_in_dim(short_w.reshape(3, 3, groups, per), me, 1, axis=2)
    taps = taps.reshape(3, 3 * per)
    extended = jnp.pad(spread.astype(jnp.float32), ((0, 0), (2, 0)))
    length = spread.shape[1]
    short = (
        taps[0][:, None] * extended[:, 2:]
        + taps[1][:, None] * extended[:, 1 : length + 1]
        + taps[2][:, None] * extended[:, :length]
    ).astype(jnp.bfloat16)
    half = SIDE // 2
    state = chain(
        short.reshape(3, per, half, SIDE),
        spectra,
        filter_bias,
        tabs,
    ).reshape(per, length)
    returned = lax.all_to_all(state, "seq", split_axis=1, concat_axis=0, tiled=True)
    return pl.pallas_call(
        out_kernel,
        out_shape=jax.ShapeDtypeStruct((returned.shape[1], w_out.shape[1]), jnp.bfloat16),
    )(returned, w_out)


def solution(mesh):
    return jax.shard_map(
        local,
        mesh=mesh,
        in_specs=(P(("win", "seq"), None), P(), P(), P(None, "seq", None), P(None, "seq"), P()),
        out_specs=P(("win", "seq"), None),
        check_vma=False,
    )
```

```python
import math

import jax
import jax.numpy as jnp
from jax import lax
from jax.experimental import pallas as pl
from jax.experimental.pallas import tpu as pltpu
from jax.sharding import PartitionSpec as P

SIDE = 256


def halves(values):
    upper = values.astype(jnp.bfloat16)
    return upper, (values - upper.astype(jnp.float32)).astype(jnp.bfloat16)


def product(left, right):
    left_hi, left_lo = halves(left)
    right_hi, right_lo = halves(right)
    total = jnp.dot(left_hi, right_hi, preferred_element_type=jnp.float32)
    total = total + jnp.dot(left_lo, right_hi, preferred_element_type=jnp.float32)
    return total + jnp.dot(left_hi, right_lo, preferred_element_type=jnp.float32)


def single(left, right):
    return jnp.dot(
        left.astype(jnp.bfloat16), right.astype(jnp.bfloat16), preferred_element_type=jnp.float32
    )


def make_tables():
    rows = lax.broadcasted_iota(jnp.int32, (SIDE, SIDE), 0)
    cols = lax.broadcasted_iota(jnp.int32, (SIDE, SIDE), 1)
    rows, cols = lax.optimization_barrier((rows, cols))
    step = -2.0 * math.pi / SIDE
    small = ((rows * cols) % SIDE).astype(jnp.float32) * step
    big = (rows * cols).astype(jnp.float32) * (step / SIDE)
    f_re, f_im = jnp.cos(small), jnp.sin(small)
    half = SIDE // 2
    left_fwd = jnp.concatenate([f_re[:, :half], f_im[:, :half]], 0)
    right_fwd = jnp.concatenate(
        [jnp.concatenate([f_re, f_im], 1), jnp.concatenate([-f_im, f_re], 1)], 0
    )
    right_inv = jnp.concatenate(
        [jnp.concatenate([f_re, -f_im], 1), jnp.concatenate([f_im, f_re], 1)], 0
    )
    left_inv = jnp.concatenate([f_re[:half], f_im[:half]], 1)
    return left_fwd, right_fwd, right_inv, left_inv, jnp.cos(big), jnp.sin(big), f_re, f_im


def spectrum(rows_in, left_fwd, right_fwd, tw_re, tw_im, mul):
    stacked = mul(left_fwd, rows_in)
    b_re, b_im = stacked[:SIDE], stacked[SIDE:]
    t_re = b_re * tw_re - b_im * tw_im
    t_im = b_re * tw_im + b_im * tw_re
    return mul(jnp.concatenate([t_re, t_im], 1), right_fwd)


def filter_kernel(filt_ref, lf_ref, rf_ref, twr_ref, twi_ref, out_ref):
    out_ref[0, 0] = spectrum(
        filt_ref[0, 0], lf_ref[...], rf_ref[...], twr_ref[...], twi_ref[...], product
    )


def filter_spectra(filters, tabs):
    left_fwd, right_fwd, _, _, tw_re, tw_im = tabs[:6]
    orders, per = filters.shape[:2]
    half = SIDE // 2
    full = lambda shape: pl.BlockSpec(shape, lambda o, c: (0,) * len(shape))
    return pl.pallas_call(
        filter_kernel,
        grid=(orders, per),
        in_specs=[
            pl.BlockSpec((1, 1, half, SIDE), lambda o, c: (o, c, 0, 0)),
            full((2 * SIDE, half)),
            full((2 * SIDE, 2 * SIDE)),
            full((SIDE, SIDE)),
            full((SIDE, SIDE)),
        ],
        out_specs=pl.BlockSpec((1, 1, SIDE, 2 * SIDE), lambda o, c: (o, c, 0, 0)),
        out_shape=jax.ShapeDtypeStruct((orders, per, SIDE, 2 * SIDE), jnp.float32),
        compiler_params=pltpu.CompilerParams(vmem_limit_bytes=16 * 1024 * 1024),
    )(filters, left_fwd, right_fwd, tw_re, tw_im)


def convolve(sig, f_spec, bias, tabs):
    left_fwd, right_fwd, right_inv, left_inv, tw_re, tw_im = tabs
    signal = sig.astype(jnp.float32)
    s_spec = spectrum(sig, left_fwd, right_fwd, tw_re, tw_im, single)
    s_re, s_im = s_spec[:, :SIDE], s_spec[:, SIDE:]
    f_re, f_im = f_spec[:, :SIDE], f_spec[:, SIDE:]
    p_re = s_re * f_re - s_im * f_im
    p_im = s_re * f_im + s_im * f_re
    d = single(jnp.concatenate([p_re, p_im], 1), right_inv)
    d_re, d_im = d[:, :SIDE], d[:, SIDE:]
    e_re = d_re * tw_re + d_im * tw_im
    e_im = d_im * tw_re - d_re * tw_im
    back = single(left_inv, jnp.concatenate([e_re, e_im], 0))
    scale = 1.0 / (SIDE * SIDE)
    return (back * scale + bias * signal).astype(jnp.bfloat16)


def chain_kernel(short_ref, spec_ref, bias_ref, fr_ref, fi_ref, twr_ref, twi_ref, out_ref):
    channel = pl.program_id(0)
    half = SIDE // 2
    f_re, f_im = fr_ref[...], fi_ref[...]
    left_fwd = jnp.concatenate([f_re[:, :half], f_im[:, :half]], 0)
    right_fwd = jnp.concatenate(
        [jnp.concatenate([f_re, f_im], 1), jnp.concatenate([-f_im, f_re], 1)], 0
    )
    right_inv = jnp.concatenate(
        [jnp.concatenate([f_re, -f_im], 1), jnp.concatenate([f_im, f_re], 1)], 0
    )
    left_inv = jnp.concatenate([f_re[:half], f_im[:half]], 1)
    tabs = (left_fwd, right_fwd, right_inv, left_inv, twr_ref[...], twi_ref[...])
    state = short_ref[2, 0]
    for order in range(2):
        conv = convolve(state, spec_ref[order, 0], bias_ref[order, channel], tabs)
        state = (short_ref[order, 0].astype(jnp.float32) * conv.astype(jnp.float32)).astype(jnp.bfloat16)
    out_ref[0] = state


def chain(short, spectra, bias, tabs):
    per = short.shape[1]
    half = SIDE // 2
    tw_re, tw_im, f_re, f_im = tabs[4:]
    full = lambda shape: pl.BlockSpec(shape, lambda c: (0,) * len(shape))
    return pl.pallas_call(
        chain_kernel,
        grid=(per,),
        in_specs=[
            pl.BlockSpec((3, 1, half, SIDE), lambda c: (0, c, 0, 0)),
            pl.BlockSpec((2, 1, SIDE, 2 * SIDE), lambda c: (0, c, 0, 0)),
            pl.BlockSpec(memory_space=pltpu.SMEM),
            full((SIDE, SIDE)),
            full((SIDE, SIDE)),
            full((SIDE, SIDE)),
            full((SIDE, SIDE)),
        ],
        out_specs=pl.BlockSpec((1, half, SIDE), lambda c: (c, 0, 0)),
        out_shape=jax.ShapeDtypeStruct((per, half, SIDE), jnp.bfloat16),
        compiler_params=pltpu.CompilerParams(vmem_limit_bytes=16 * 1024 * 1024),
    )(short, spectra, bias, f_re.astype(jnp.bfloat16), f_im.astype(jnp.bfloat16), tw_re, tw_im)


def local(layer_input, w_in, short_w, filters, filter_bias, w_out):
    width = w_out.shape[0]
    groups = lax.axis_size("seq")
    per = width // groups
    projected = lax.dot_general(
        w_in, layer_input, (((0,), (1,)), ((), ())), preferred_element_type=jnp.float32
    ).astype(jnp.bfloat16)
    positions = projected.shape[1]
    grouped = jnp.swapaxes(projected.reshape(3, groups, per, positions), 0, 1)
    tabs = make_tables()
    spectra = filter_spectra(filters.reshape(2, per, SIDE // 2, SIDE), tabs)
    spread = lax.all_to_all(
        grouped.reshape(groups, 3 * per, positions), "seq", split_axis=0, concat_axis=2, tiled=True
    ).reshape(3 * per, groups * positions)
    me = lax.axis_index("seq")
    taps = lax.dynamic_slice_in_dim(short_w.reshape(3, 3, groups, per), me, 1, axis=2)
    taps = taps.reshape(3, 3 * per)
    extended = jnp.pad(spread.astype(jnp.float32), ((0, 0), (2, 0)))
    length = spread.shape[1]
    short = (
        taps[0][:, None] * extended[:, 2:]
        + taps[1][:, None] * extended[:, 1 : length + 1]
        + taps[2][:, None] * extended[:, :length]
    ).astype(jnp.bfloat16)
    half = SIDE // 2
    state = chain(
        short.reshape(3, per, half, SIDE),
        spectra,
        filter_bias,
        tabs,
    ).reshape(per, length)
    returned = lax.all_to_all(state, "seq", split_axis=1, concat_axis=0, tiled=True)
    output = lax.dot_general(
        returned, w_out, (((0,), (0,)), ((), ())), preferred_element_type=jnp.float32
    )
    return output.astype(jnp.bfloat16)


def solution(mesh):
    return jax.shard_map(
        local,
        mesh=mesh,
        in_specs=(P(("win", "seq"), None), P(), P(), P(None, "seq", None), P(None, "seq"), P()),
        out_specs=P(("win", "seq"), None),
        check_vma=False,
    )
```

```python
import math

import jax
import jax.numpy as jnp
from jax import lax
from jax.experimental import pallas as pl
from jax.experimental.pallas import tpu as pltpu
from jax.sharding import PartitionSpec as P

SIDE = 256


def halves(values):
    upper = values.astype(jnp.bfloat16)
    return upper, (values - upper.astype(jnp.float32)).astype(jnp.bfloat16)


def product(left, right):
    left_hi, left_lo = halves(left)
    right_hi, right_lo = halves(right)
    total = jnp.dot(left_hi, right_hi, preferred_element_type=jnp.float32)
    return total + jnp.dot(left_lo, right_hi, preferred_element_type=jnp.float32)


def single(left, right):
    return jnp.dot(
        left.astype(jnp.bfloat16), right.astype(jnp.bfloat16), preferred_element_type=jnp.float32
    )


def make_tables():
    rows = lax.broadcasted_iota(jnp.int32, (SIDE, SIDE), 0)
    cols = lax.broadcasted_iota(jnp.int32, (SIDE, SIDE), 1)
    rows, cols = lax.optimization_barrier((rows, cols))
    step = -2.0 * math.pi / SIDE
    small = ((rows * cols) % SIDE).astype(jnp.float32) * step
    big = (rows * cols).astype(jnp.float32) * (step / SIDE)
    f_re, f_im = jnp.cos(small), jnp.sin(small)
    half = SIDE // 2
    left_fwd = jnp.concatenate([f_re[:, :half], f_im[:, :half]], 0)
    right_fwd = jnp.concatenate(
        [jnp.concatenate([f_re, f_im], 1), jnp.concatenate([-f_im, f_re], 1)], 0
    )
    right_inv = jnp.concatenate(
        [jnp.concatenate([f_re, -f_im], 1), jnp.concatenate([f_im, f_re], 1)], 0
    )
    left_inv = jnp.concatenate([f_re[:half], f_im[:half]], 1)
    return left_fwd, right_fwd, right_inv, left_inv, jnp.cos(big), jnp.sin(big), f_re, f_im


def spectrum(rows_in, left_fwd, right_fwd, tw_re, tw_im, mul):
    stacked = mul(left_fwd, rows_in)
    b_re, b_im = stacked[:SIDE], stacked[SIDE:]
    t_re = b_re * tw_re - b_im * tw_im
    t_im = b_re * tw_im + b_im * tw_re
    return mul(jnp.concatenate([t_re, t_im], 1), right_fwd)


def filter_kernel(filt_ref, lf_ref, rf_ref, twr_ref, twi_ref, out_ref):
    out_ref[0, 0] = spectrum(
        filt_ref[0, 0], lf_ref[...], rf_ref[...], twr_ref[...], twi_ref[...], product
    )


def filter_spectra(filters, tabs):
    left_fwd, right_fwd, _, _, tw_re, tw_im = tabs[:6]
    orders, per = filters.shape[:2]
    half = SIDE // 2
    full = lambda shape: pl.BlockSpec(shape, lambda o, c: (0,) * len(shape))
    return pl.pallas_call(
        filter_kernel,
        grid=(orders, per),
        in_specs=[
            pl.BlockSpec((1, 1, half, SIDE), lambda o, c: (o, c, 0, 0)),
            full((2 * SIDE, half)),
            full((2 * SIDE, 2 * SIDE)),
            full((SIDE, SIDE)),
            full((SIDE, SIDE)),
        ],
        out_specs=pl.BlockSpec((1, 1, SIDE, 2 * SIDE), lambda o, c: (o, c, 0, 0)),
        out_shape=jax.ShapeDtypeStruct((orders, per, SIDE, 2 * SIDE), jnp.float32),
        compiler_params=pltpu.CompilerParams(vmem_limit_bytes=48 * 1024 * 1024),
    )(filters, left_fwd, right_fwd, tw_re, tw_im)


def convolve(sig, f_spec, bias, tabs):
    left_fwd, right_fwd, right_inv, left_inv, tw_re, tw_im = tabs
    signal = sig.astype(jnp.float32)
    s_spec = spectrum(sig, left_fwd, right_fwd, tw_re, tw_im, single)
    s_re, s_im = s_spec[:, :SIDE], s_spec[:, SIDE:]
    f_re, f_im = f_spec[:, :SIDE], f_spec[:, SIDE:]
    p_re = s_re * f_re - s_im * f_im
    p_im = s_re * f_im + s_im * f_re
    d = single(jnp.concatenate([p_re, p_im], 1), right_inv)
    d_re, d_im = d[:, :SIDE], d[:, SIDE:]
    e_re = d_re * tw_re + d_im * tw_im
    e_im = d_im * tw_re - d_re * tw_im
    back = single(left_inv, jnp.concatenate([e_re, e_im], 0))
    scale = 1.0 / (SIDE * SIDE)
    return (back * scale + bias * signal).astype(jnp.bfloat16)


def chain_kernel(short_ref, spec_ref, bias_ref, fr_ref, fi_ref, twr_ref, twi_ref, out_ref):
    channel = pl.program_id(0)
    half = SIDE // 2
    f_re, f_im = fr_ref[...], fi_ref[...]
    left_fwd = jnp.concatenate([f_re[:, :half], f_im[:, :half]], 0)
    right_fwd = jnp.concatenate(
        [jnp.concatenate([f_re, f_im], 1), jnp.concatenate([-f_im, f_re], 1)], 0
    )
    right_inv = jnp.concatenate(
        [jnp.concatenate([f_re, -f_im], 1), jnp.concatenate([f_im, f_re], 1)], 0
    )
    left_inv = jnp.concatenate([f_re[:half], f_im[:half]], 1)
    tabs = (left_fwd, right_fwd, right_inv, left_inv, twr_ref[...], twi_ref[...])
    state = short_ref[2, 0]
    for order in range(2):
        conv = convolve(state, spec_ref[order, 0], bias_ref[order, channel], tabs)
        state = (short_ref[order, 0].astype(jnp.float32) * conv.astype(jnp.float32)).astype(jnp.bfloat16)
    out_ref[0] = state


def chain(short, spectra, bias, tabs):
    per = short.shape[1]
    half = SIDE // 2
    tw_re, tw_im, f_re, f_im = tabs[4:]
    full = lambda shape: pl.BlockSpec(shape, lambda c: (0,) * len(shape))
    return pl.pallas_call(
        chain_kernel,
        grid=(per,),
        in_specs=[
            pl.BlockSpec((3, 1, half, SIDE), lambda c: (0, c, 0, 0)),
            pl.BlockSpec((2, 1, SIDE, 2 * SIDE), lambda c: (0, c, 0, 0)),
            pl.BlockSpec(memory_space=pltpu.SMEM),
            full((SIDE, SIDE)),
            full((SIDE, SIDE)),
            full((SIDE, SIDE)),
            full((SIDE, SIDE)),
        ],
        out_specs=pl.BlockSpec((1, half, SIDE), lambda c: (c, 0, 0)),
        out_shape=jax.ShapeDtypeStruct((per, half, SIDE), jnp.bfloat16),
        compiler_params=pltpu.CompilerParams(vmem_limit_bytes=48 * 1024 * 1024),
    )(short, spectra, bias, f_re.astype(jnp.bfloat16), f_im.astype(jnp.bfloat16), tw_re, tw_im)


def local(layer_input, w_in, short_w, filters, filter_bias, w_out):
    width = w_out.shape[0]
    groups = lax.axis_size("seq")
    per = width // groups
    projected = lax.dot_general(
        w_in, layer_input, (((0,), (1,)), ((), ())), preferred_element_type=jnp.float32
    ).astype(jnp.bfloat16)
    positions = projected.shape[1]
    grouped = jnp.swapaxes(projected.reshape(3, groups, per, positions), 0, 1)
    tabs = make_tables()
    spectra = filter_spectra(filters.reshape(2, per, SIDE // 2, SIDE), tabs)
    spread = lax.all_to_all(
        grouped.reshape(groups, 3 * per, positions), "seq", split_axis=0, concat_axis=2, tiled=True
    ).reshape(3 * per, groups * positions)
    me = lax.axis_index("seq")
    taps = lax.dynamic_slice_in_dim(short_w.reshape(3, 3, groups, per), me, 1, axis=2)
    taps = taps.reshape(3, 3 * per)
    extended = jnp.pad(spread.astype(jnp.float32), ((0, 0), (2, 0)))
    length = spread.shape[1]
    short = (
        taps[0][:, None] * extended[:, 2:]
        + taps[1][:, None] * extended[:, 1 : length + 1]
        + taps[2][:, None] * extended[:, :length]
    ).astype(jnp.bfloat16)
    half = SIDE // 2
    state = chain(
        short.reshape(3, per, half, SIDE),
        spectra,
        filter_bias,
        tabs,
    ).reshape(per, length)
    returned = lax.all_to_all(state, "seq", split_axis=1, concat_axis=0, tiled=True)
    output = lax.dot_general(
        returned, w_out, (((0,), (0,)), ((), ())), preferred_element_type=jnp.float32
    )
    return output.astype(jnp.bfloat16)


def solution(mesh):
    return jax.shard_map(
        local,
        mesh=mesh,
        in_specs=(P(("win", "seq"), None), P(), P(), P(None, "seq", None), P(None, "seq"), P()),
        out_specs=P(("win", "seq"), None),
        check_vma=False,
    )
```
